32 devices in a mesh: groups: 2 (over x), dp: 16 (over z, y, core).
Axes of the slice: x: 2, y: 2, z: 4, core: 2. Of those that a mesh axis runs over, the one named last changes fastest.
Arguments:
- hidden: bfloat16 [12288, 11008], P(('groups', 'dp')), parts along dimension 0, may hold values from -6 to 6
- out_grad: bfloat16 [12288, 4096], P(('groups', 'dp')), parts along dimension 0, may hold values from -0.75 to 0.75
- hidden_basis: bfloat16 [64, 11008], P(None, 'dp'), may hold values from -0.0546875 to 0.0546875
- output_basis: bfloat16 [64, 4096], P(None, 'dp'), may hold values from -0.09375 to 0.09375
- owner_ids: int32 [12288, 1], P(('groups', 'dp')), parts along dimension 0, may hold values from 0 to 15; in each aligned block of 384 rows (0 to 383, 384 to 767, ...) at most 48 rows name the same one
- doc_slot: int32 [12288], P(('groups', 'dp')), parts along dimension 0, may hold values from 0 to 7
Outputs:
- doc_grads: float32 [256, 4096], P(('groups', 'dp')), parts along dimension 0
The draws below stay inside these ranges and needn't reach their ends.
There are 2 independent parts, one for each index of `groups`. The reference program is written for one: setup_inputs(seed, part) draws one part's arguments, and reference() takes and returns one part's arrays. A program takes and returns all parts, laid end to end along the dimension named above; an argument that names none is the same for every part. Nothing has to cross between parts.
Inputs may be any that keep to these rules, and one draw needn't show every extreme that they name: `owner_ids`: among the 384 tokens of one device, at most 48 have the same owner, and some owner gets exactly 48 of them.
All inputs are finite; a program needn't handle non-finite values.
Results may differ from the reference program's by a relative error of at most 0.0042.
Values may be sent and summed in bfloat16 or wider, within the bound.
No kernel may reach another device: no remote copies, remote signals or barrier semaphores. Data moves between devices by JAX's collectives and lax.ppermute only.
A program may use at most 128 MiB of HBM per device.

```python
import math
import jax
import jax.numpy as jnp
import numpy as np

D = 4096
FF = 11008
RANK = 64
TOK_DEV = 384
DOCS_DEV = 8
CAP = 48
TOKENS = 6144
N_DP = 16


def place_ends(drawn, own_key, smallest, top_value):
    longest = drawn.shape.index(max(drawn.shape))
    spots = []
    for shift in (0, 1):
        where = [jax.random.randint(jax.random.fold_in(own_key, axis), (), 0, length) for axis, length in enumerate(drawn.shape)]
        where[longest] = (where[longest] + shift) % drawn.shape[longest]
        spots.append(tuple(where))
    return drawn.at[spots[0]].set(smallest).at[spots[1]].set(top_value)


def level_of(key, extent, split, smallest, top_value):
    loudness = 1.0
    for axis_at, parts in split:
        steps = jax.random.uniform(jax.random.fold_in(jax.random.fold_in(key, 6), axis_at), (parts,), jnp.float32, smallest / len(split), top_value / len(split))
        loudness = loudness * jnp.repeat(jnp.exp(steps), extent[axis_at] // parts).reshape((-1,) + (1,) * (len(extent) - 1 - axis_at))
    return loudness


def routed_block(stream_key, own, number, rows, amount, top, limit, skew):
    order = jax.random.permutation(stream_key, amount)
    crowded, ordinary = load_shares(amount, rows * top, limit, skew, True), load_shares(amount, rows * top, limit, skew, False)
    places = jnp.arange(amount)

    def named(lengths, rotation):
        used = int((lengths > 0).sum())
        fixed = max(1, used // 4)
        moved = fixed + (places - fixed + rotation * (used - fixed)) % max(1, amount - fixed)
        return jnp.zeros((amount,), jnp.int32).at[order[jnp.where(places < fixed, places, moved)]].set(jnp.asarray(lengths, jnp.int32))

    lengths = jnp.where(number % 4 == 0, named(crowded, number // 4), named(ordinary, number - number // 4 - 1))
    mixed = jax.random.permutation(jax.random.fold_in(own, 3), amount)
    donor, sink = mixed[0:amount // 2 * 2:2], mixed[1:amount // 2 * 2:2]
    room = jnp.minimum(lengths[donor] - 1, limit - lengths[sink]) // 2
    room = jnp.where((donor == order[0]) | (sink == order[0]) | (lengths[sink] == 0), 0, jnp.maximum(room, 0))
    moved = jax.random.randint(jax.random.fold_in(own, 4), (amount // 2,), 0, 1 << 20) % (room + 1)
    lengths = lengths.at[donor].add(-moved).at[sink].add(moved)
    labels = jnp.searchsorted(jnp.cumsum(lengths), jnp.arange(rows * top), side="right").astype(jnp.int32)
    table = labels.reshape(top, rows).T
    table = table[jax.random.permutation(jax.random.fold_in(own, 1), rows)]
    rotation = jax.random.randint(jax.random.fold_in(own, 2), (rows, 1), 0, top)
    return jnp.take_along_axis(table, (jnp.arange(top)[None, :] + rotation) % top, axis=1)


def load_shares(count, total, most, skew, full):
    loads = [(1 << 20) // math.isqrt(grade ** skew) + 1 for grade in range(1, count + 1)]
    largest = most if full else min(most, max(-(-total // count), total * loads[0] // sum(loads)))
    least = 1 if total - largest >= count - 1 else 0
    holding, spare = [largest] + [least] * (count - 1), total - largest - least * (count - 1)
    while spare > 0:
        candidates = [i for i in range(1, count) if holding[i] < largest] or [i for i in range(1, count) if holding[i] < most]
        pool, remaining = sum([loads[i] for i in candidates]), spare
        for i in candidates:
            extra = min(most - holding[i], max(1, remaining * loads[i] // pool), spare)
            holding[i] = holding[i] + extra
            spare = spare - extra
    return np.array(holding)


def centred(rng, dims, width, bound, pieces=(), held_as=jnp.bfloat16):
    entries = jax.random.normal(rng, dims, jnp.float32) * width
    if len(pieces) > 0:
        entries = level_of(rng, dims, pieces, -0.22, 0.18) * entries
    return jnp.clip(entries, min=-bound, max=bound).astype(held_as)


def setup_inputs(seed: int = 0, part: int = 0) -> dict:
    arg_keys = jax.random.split(jax.random.key(seed), 7)
    own_keys = jax.random.split(jax.random.fold_in(arg_keys[6], part), 7)
    hidden = centred(own_keys[0], (TOKENS, FF), 1.0, 6.0, ((0, 16),))
    out_grad = centred(own_keys[1], (TOKENS, D), 0.125, 0.75, ((0, 16),))
    hidden_basis = centred(arg_keys[2], (RANK, FF), FF ** -0.5, 0.0546875, ((1, 16),))
    output_basis = centred(arg_keys[3], (RANK, D), D ** -0.5, 0.09375, ((1, 16),))
    owner_ids_keys = jax.random.split(jax.random.fold_in(own_keys[4], 1), TOKENS // TOK_DEV)
    owner_ids_turns = jax.random.permutation(jax.random.fold_in(own_keys[4], 3), TOKENS // TOK_DEV)
    owner_ids = jax.vmap(lambda own, number: routed_block(jax.random.fold_in(own_keys[4], 2), own, number, TOK_DEV, N_DP, 1, CAP, 2))(owner_ids_keys, owner_ids_turns).reshape((TOKENS, 1))
    doc_slot = place_ends(jax.random.randint(own_keys[5], (TOKENS,), 0, DOCS_DEV), jax.random.fold_in(own_keys[5], 1), 0, DOCS_DEV - 1).astype(jnp.int32)
    return dict(hidden=hidden, out_grad=out_grad, hidden_basis=hidden_basis, output_basis=output_basis, owner_ids=owner_ids, doc_slot=doc_slot)


def reference(hidden, out_grad, hidden_basis, output_basis, owner_ids, doc_slot):
    doc = (owner_ids[:, 0] * DOCS_DEV + doc_slot).astype(jnp.int32)
    left = jnp.dot(hidden, hidden_basis.T, preferred_element_type=jnp.float32).astype(jnp.bfloat16)
    right = jnp.dot(out_grad, output_basis.T, preferred_element_type=jnp.float32).astype(jnp.bfloat16)
    left_wide = left.astype(jnp.float32)
    right_wide = right.astype(jnp.float32)
    outer = (left_wide[:, :, None] * right_wide[:, None, :]).reshape(left.shape[0], RANK * RANK)
    return jax.ops.segment_sum(outer, doc, num_segments=DOCS_DEV * N_DP)
```

```python
import jax
import jax.numpy as jnp
from jax import lax
from jax.sharding import PartitionSpec as P

DOCS_DEV = 8


def gather_bases(hidden_basis, output_basis, devices):
    rank_width, hidden_cols = hidden_basis.shape
    packed = jnp.concatenate([hidden_basis, output_basis], axis=1)[None]
    spread = jnp.broadcast_to(packed, (devices,) + packed.shape[1:])
    got = lax.all_to_all(spread, "dp", 0, 0, tiled=True)
    hidden_full = got[:, :, :hidden_cols].transpose(1, 0, 2).reshape(rank_width, -1)
    output_full = got[:, :, hidden_cols:].transpose(1, 0, 2).reshape(rank_width, -1)
    return hidden_full, output_full


def project(token_block, basis):
    summed = lax.dot_general(
        token_block, basis, (((1,), (1,)), ((), ())), preferred_element_type=jnp.float32
    )
    return summed.astype(jnp.bfloat16)


def local(hidden, out_grad, hidden_basis, output_basis, owner_ids, doc_slot):
    devices = lax.axis_size("dp")
    local_tokens = hidden.shape[0]
    capacity = 2 * local_tokens // devices
    rank_width = hidden_basis.shape[0]
    buffer_len = devices * capacity
    hidden_full, output_full = gather_bases(hidden_basis, output_basis, devices)
    left = project(hidden, hidden_full)
    right = project(out_grad, output_full)
    targets = owner_ids[:, 0]
    member = (targets[:, None] == jnp.arange(devices, dtype=jnp.int32)[None, :]).astype(jnp.bfloat16)
    token_ids = jnp.arange(local_tokens, dtype=jnp.int32)
    earlier = (token_ids[:, None] > token_ids[None, :]).astype(jnp.bfloat16)
    before = lax.dot_general(
        earlier, member, (((1,), (0,)), ((), ())), preferred_element_type=jnp.float32
    )
    position = jnp.sum(member.astype(jnp.float32) * before, axis=1).astype(jnp.int32)
    slot_index = targets * capacity + position
    dispatch = (
        jnp.arange(buffer_len, dtype=jnp.int32)[:, None] == slot_index[None, :]
    ).astype(jnp.bfloat16)
    label = (doc_slot + 1).astype(jnp.bfloat16)[:, None]
    rows = jnp.concatenate([left, right, label], axis=1)
    buffer = lax.dot_general(
        dispatch, rows, (((1,), (0,)), ((), ())), preferred_element_type=jnp.float32
    ).astype(jnp.bfloat16)
    arrived = lax.all_to_all(buffer, "dp", 0, 0, tiled=True)
    left_in = arrived[:, :rank_width]
    right_in = arrived[:, rank_width:2 * rank_width]
    label_in = arrived[:, 2 * rank_width:]
    selector = (label_in == (jnp.arange(DOCS_DEV, dtype=jnp.int32) + 1)[None, :].astype(jnp.bfloat16)).astype(
        jnp.bfloat16
    )
    weighted = (selector[:, :, None] * left_in[:, None, :]).reshape(buffer_len, DOCS_DEV * rank_width)
    grads = lax.dot_general(
        weighted, right_in, (((0,), (0,)), ((), ())), preferred_element_type=jnp.float32
    )
    return grads.reshape(DOCS_DEV, rank_width * rank_width)


def solution(mesh):
    placed = (
        P(("groups", "dp"), None),
        P(("groups", "dp"), None),
        P(None, "dp"),
        P(None, "dp"),
        P(("groups", "dp"), None),
        P(("groups", "dp")),
    )
    return jax.shard_map(
        local, mesh=mesh, in_specs=placed, out_specs=P(("groups", "dp"), None), check_vma=False
    )
```

```python
import numpy as np
import jax
import jax.numpy as jnp
from jax import lax
from jax.sharding import PartitionSpec as P

DOCS_DEV = 8


def ring_planes(devices):
    chips = devices // 2
    if devices % 2 or chips < 2:
        return [list(range(devices))]
    if chips % 2 == 0 and chips >= 4:
        order = list(range(0, chips, 2)) + list(range(chips - 1, 0, -2))
    else:
        order = list(range(chips))
    return [[2 * chip + core for chip in order] for core in range(2)]


def ring_gather(block, devices):
    planes = ring_planes(devices)
    length = len(planes[0])
    me = lax.axis_index("dp")
    place = np.zeros(devices, np.int32)
    plane_of = np.zeros(devices, np.int32)
    for plane, members in enumerate(planes):
        for spot, member in enumerate(members):
            place[member] = spot
            plane_of[member] = plane
    spot = jnp.asarray(place)[me]
    forward = [(ring[t], ring[(t + 1) % length]) for ring in planes for t in range(length)]
    backward = [(ring[t], ring[(t - 1) % length]) for ring in planes for t in range(length)]
    ahead = [block]
    behind = []
    moving = block
    for _ in range(length // 2):
        moving = lax.ppermute(moving, "dp", forward)
        ahead.append(moving)
    moving = block
    for _ in range(length - 1 - length // 2):
        moving = lax.ppermute(moving, "dp", backward)
        behind.append(moving)
    by_distance = jnp.stack(ahead + behind[::-1])
    mine = by_distance[(spot - jnp.arange(length)) % length]
    if len(planes) == 1:
        stacks = [mine]
    else:
        swap = list(zip(planes[0], planes[1])) + list(zip(planes[1], planes[0]))
        other = lax.ppermute(mine, "dp", swap)
        first = jnp.asarray(plane_of)[me] == 0
        stacks = [jnp.where(first, mine, other), jnp.where(first, other, mine)]
    pieces = [None] * devices
    for plane, members in enumerate(planes):
        for at, member in enumerate(members):
            pieces[member] = stacks[plane][at]
    return pieces


def project(token_block, basis):
    summed = lax.dot_general(
        token_block, basis, (((1,), (1,)), ((), ())), preferred_element_type=jnp.float32
    )
    return summed.astype(jnp.bfloat16)


def local(hidden, out_grad, hidden_basis, output_basis, owner_ids, doc_slot):
    devices = lax.axis_size("dp")
    local_tokens = hidden.shape[0]
    capacity = 2 * local_tokens // devices
    rank_width = hidden_basis.shape[0]
    hidden_cols = hidden_basis.shape[1]
    buffer_len = devices * capacity
    pieces = ring_gather(jnp.concatenate([hidden_basis, output_basis], axis=1), devices)
    hidden_full = jnp.concatenate([piece[:, :hidden_cols] for piece in pieces], axis=1)
    output_full = jnp.concatenate([piece[:, hidden_cols:] for piece in pieces], axis=1)
    left = project(hidden, hidden_full)
    right = project(out_grad, output_full)
    targets = owner_ids[:, 0]
    member = (targets[:, None] == jnp.arange(devices, dtype=jnp.int32)[None, :]).astype(jnp.bfloat16)
    token_ids = jnp.arange(local_tokens, dtype=jnp.int32)
    earlier = (token_ids[:, None] > token_ids[None, :]).astype(jnp.bfloat16)
    before = lax.dot_general(
        earlier, member, (((1,), (0,)), ((), ())), preferred_element_type=jnp.float32
    )
    position = jnp.sum(member.astype(jnp.float32) * before, axis=1).astype(jnp.int32)
    slot_index = targets * capacity + position
    dispatch = (
        jnp.arange(buffer_len, dtype=jnp.int32)[:, None] == slot_index[None, :]
    ).astype(jnp.bfloat16)
    rows = jnp.concatenate([left, right], axis=1)
    buffer = lax.dot_general(
        dispatch, rows, (((1,), (0,)), ((), ())), preferred_element_type=jnp.float32
    ).astype(jnp.bfloat16)
    label = lax.dot_general(
        dispatch, (doc_slot + 1).astype(jnp.bfloat16), (((1,), (0,)), ((), ())),
        preferred_element_type=jnp.float32,
    ).astype(jnp.bfloat16)
    width = 2 * rank_width
    label_row = jnp.pad(label.reshape(devices, 1, capacity), ((0, 0), (0, 0), (0, width - capacity)))
    packed = jnp.concatenate([buffer.reshape(devices, capacity, width), label_row], axis=1)
    arrived = lax.all_to_all(packed, "dp", 0, 0, tiled=True)
    rows_in = arrived[:, :capacity, :].reshape(buffer_len, width)
    label_in = arrived[:, capacity, :capacity].reshape(buffer_len, 1)
    left_in = rows_in[:, :rank_width]
    right_in = rows_in[:, rank_width:]
    wanted = (jnp.arange(DOCS_DEV, dtype=jnp.int32) + 1).astype(jnp.bfloat16)[None, :]
    selector = (label_in == wanted).astype(jnp.bfloat16)
    weighted = (selector[:, :, None] * left_in[:, None, :]).reshape(buffer_len, DOCS_DEV * rank_width)
    grads = lax.dot_general(
        weighted, right_in, (((0,), (0,)), ((), ())), preferred_element_type=jnp.float32
    )
    return grads.reshape(DOCS_DEV, rank_width * rank_width)


def solution(mesh):
    placed = (
        P(("groups", "dp"), None),
        P(("groups", "dp"), None),
        P(None, "dp"),
        P(None, "dp"),
        P(("groups", "dp"), None),
        P(("groups", "dp")),
    )
    return jax.shard_map(
        local, mesh=mesh, in_specs=placed, out_specs=P(("groups", "dp"), None), check_vma=False
    )
```

```python
import numpy as np
import jax
import jax.numpy as jnp
from jax import lax
from jax.sharding import PartitionSpec as P

DOCS_DEV = 8


def ring_planes(devices):
    chips = devices // 2
    if devices % 2 or chips < 2:
        return [list(range(devices))]
    if chips % 2 == 0 and chips >= 4:
        order = list(range(0, chips, 2)) + list(range(chips - 1, 0, -2))
    else:
        order = list(range(chips))
    return [[2 * chip + core for chip in order] for core in range(2)]


def ring_gather(block, devices):
    planes = ring_planes(devices)
    length = len(planes[0])
    me = lax.axis_index("dp")
    place = np.zeros(devices, np.int32)
    plane_of = np.zeros(devices, np.int32)
    for plane, members in enumerate(planes):
        for spot, member in enumerate(members):
            place[member] = spot
            plane_of[member] = plane
    spot = jnp.asarray(place)[me]
    forward = [(ring[t], ring[(t + 1) % length]) for ring in planes for t in range(length)]
    backward = [(ring[t], ring[(t - 1) % length]) for ring in planes for t in range(length)]
    ahead = [block]
    behind = []
    moving = block
    for _ in range(length // 2):
        moving = lax.ppermute(moving, "dp", forward)
        ahead.append(moving)
    moving = block
    for _ in range(length - 1 - length // 2):
        moving = lax.ppermute(moving, "dp", backward)
        behind.append(moving)
    by_distance = jnp.stack(ahead + behind[::-1])
    chip_spot = np.zeros(length, np.int32)
    for at, member in enumerate(planes[0]):
        chip_spot[member // len(planes)] = at
    mine = by_distance[(spot - jnp.asarray(chip_spot)) % length]
    if len(planes) == 1:
        return mine
    swap = list(zip(planes[0], planes[1])) + list(zip(planes[1], planes[0]))
    other = lax.ppermute(mine, "dp", swap)
    first = jnp.asarray(plane_of)[me] == 0
    both = jnp.where(first, jnp.stack([mine, other], axis=1), jnp.stack([other, mine], axis=1))
    return both.reshape((devices,) + block.shape)


def project(token_block, basis):
    summed = lax.dot_general(
        token_block, basis, (((1,), (1,)), ((), ())), preferred_element_type=jnp.float32
    )
    return summed.astype(jnp.bfloat16)


def local(hidden, out_grad, hidden_basis, output_basis, owner_ids, doc_slot):
    devices = lax.axis_size("dp")
    local_tokens = hidden.shape[0]
    capacity = 2 * local_tokens // devices
    rank_width = hidden_basis.shape[0]
    hidden_cols = hidden_basis.shape[1]
    buffer_len = devices * capacity
    stacked = ring_gather(jnp.concatenate([hidden_basis, output_basis], axis=1), devices)
    hidden_full = stacked[:, :, :hidden_cols].transpose(1, 0, 2).reshape(rank_width, -1)
    output_full = stacked[:, :, hidden_cols:].transpose(1, 0, 2).reshape(rank_width, -1)
    left = project(hidden, hidden_full)
    right = project(out_grad, output_full)
    targets = owner_ids[:, 0]
    member = (targets[:, None] == jnp.arange(devices, dtype=jnp.int32)[None, :]).astype(jnp.bfloat16)
    token_ids = jnp.arange(local_tokens, dtype=jnp.int32)
    earlier = (token_ids[:, None] > token_ids[None, :]).astype(jnp.bfloat16)
    before = lax.dot_general(
        earlier, member, (((1,), (0,)), ((), ())), preferred_element_type=jnp.float32
    )
    position = jnp.sum(member.astype(jnp.float32) * before, axis=1).astype(jnp.int32)
    slot_index = targets * capacity + position
    dispatch = (
        jnp.arange(buffer_len, dtype=jnp.int32)[:, None] == slot_index[None, :]
    ).astype(jnp.bfloat16)
    rows = jnp.concatenate([left, right], axis=1)
    buffer = lax.dot_general(
        dispatch, rows, (((1,), (0,)), ((), ())), preferred_element_type=jnp.float32
    ).astype(jnp.bfloat16)
    label = lax.dot_general(
        dispatch, (doc_slot + 1).astype(jnp.bfloat16), (((1,), (0,)), ((), ())),
        preferred_element_type=jnp.float32,
    ).astype(jnp.bfloat16)
    width = 2 * rank_width
    label_row = jnp.pad(label.reshape(devices, 1, capacity), ((0, 0), (0, 0), (0, width - capacity)))
    packed = jnp.concatenate([buffer.reshape(devices, capacity, width), label_row], axis=1)
    arrived = lax.all_to_all(packed, "dp", 0, 0, tiled=True)
    rows_in = arrived[:, :capacity, :].reshape(buffer_len, width)
    label_in = arrived[:, capacity, :capacity].reshape(buffer_len, 1)
    left_in = rows_in[:, :rank_width]
    right_in = rows_in[:, rank_width:]
    wanted = (jnp.arange(DOCS_DEV, dtype=jnp.int32) + 1).astype(jnp.bfloat16)[None, :]
    selector = (label_in == wanted).astype(jnp.bfloat16)
    weighted = (selector[:, :, None] * left_in[:, None, :]).reshape(buffer_len, DOCS_DEV * rank_width)
    grads = lax.dot_general(
        weighted, right_in, (((0,), (0,)), ((), ())), preferred_element_type=jnp.float32
    )
    return grads.reshape(DOCS_DEV, rank_width * rank_width)


def solution(mesh):
    placed = (
        P(("groups", "dp"), None),
        P(("groups", "dp"), None),
        P(None, "dp"),
        P(None, "dp"),
        P(("groups", "dp"), None),
        P(("groups", "dp")),
    )
    return jax.shard_map(
        local, mesh=mesh, in_specs=placed, out_specs=P(("groups", "dp"), None), check_vma=False
    )
```

```python
import numpy as np
import jax
import jax.numpy as jnp
from jax import lax
from jax.experimental import pallas as pl
from jax.experimental.pallas import tpu as pltpu
from jax.sharding import PartitionSpec as P

DOCS_DEV = 8


def ring_planes(devices):
    chips = devices // 2
    if devices % 2 or chips < 2:
        return [list(range(devices))]
    if chips % 2 == 0 and chips >= 4:
        order = list(range(0, chips, 2)) + list(range(chips - 1, 0, -2))
    else:
        order = list(range(chips))
    return [[2 * chip + core for chip in order] for core in range(2)]


def ring_gather(block, devices):
    planes = ring_planes(devices)
    length = len(planes[0])
    me = lax.axis_index("dp")
    place = np.zeros(devices, np.int32)
    plane_of = np.zeros(devices, np.int32)
    for plane, members in enumerate(planes):
        for spot, member in enumerate(members):
            place[member] = spot
            plane_of[member] = plane
    spot = jnp.asarray(place)[me]
    plane = jnp.asarray(plane_of)[me]
    forward = [(ring[t], ring[(t + 1) % length]) for ring in planes for t in range(length)]
    backward = [(ring[t], ring[(t - 1) % length]) for ring in planes for t in range(length)]
    blocks = [block]
    shifts = [0]
    moving = block
    for step in range(1, length // 2 + 1):
        moving = lax.ppermute(moving, "dp", forward)
        blocks.append(moving)
        shifts.append(-step)
    moving = block
    for step in range(1, length - length // 2):
        moving = lax.ppermute(moving, "dp", backward)
        blocks.append(moving)
        shifts.append(step)
    ring_table = jnp.asarray(np.array(planes, np.int32))
    owners = [ring_table[plane, (spot + shift) % length] for shift in shifts]
    if len(planes) > 1:
        swap = list(zip(planes[0], planes[1])) + list(zip(planes[1], planes[0]))
        blocks = blocks + [lax.ppermute(got, "dp", swap) for got in blocks]
        owners = owners + [ring_table[1 - plane, (spot + shift) % length] for shift in shifts]
    return blocks, jnp.stack(owners).astype(jnp.int32)


def projection_kernel(count, hidden_cols, output_cols, rank_width):
    def kernel(owners, *refs):
        blocks = refs[:count]
        hidden_ref, grad_ref, rows_ref, stacked, hidden_full, output_full = refs[count:]

        @pl.when(pl.program_id(0) == 0)
        def _():
            for k in range(count):
                stacked[owners[k]] = blocks[k][...]
            for d in range(count):
                hidden_full[:, d * hidden_cols:(d + 1) * hidden_cols] = stacked[d, :, :hidden_cols]
                output_full[:, d * output_cols:(d + 1) * output_cols] = stacked[d, :, hidden_cols:]

        dims = (((1,), (1,)), ((), ()))
        left = lax.dot_general(hidden_ref[...], hidden_full[...], dims, preferred_element_type=jnp.float32)
        right = lax.dot_general(grad_ref[...], output_full[...], dims, preferred_element_type=jnp.float32)
        rows_ref[:, :rank_width] = left.astype(jnp.bfloat16)
        rows_ref[:, rank_width:] = right.astype(jnp.bfloat16)

    return kernel


def project_rows(blocks, owners, hidden, out_grad):
    count = len(blocks)
    rank_width, width = blocks[0].shape
    local_tokens, features = hidden.shape
    outputs = out_grad.shape[1]
    tile = 128 if local_tokens % 128 == 0 else local_tokens
    whole = pl.BlockSpec((rank_width, width), lambda i, owners: (0, 0))
    grid_spec = pltpu.PrefetchScalarGridSpec(
        num_scalar_prefetch=1,
        grid=(local_tokens // tile,),
        in_specs=[whole] * count + [
            pl.BlockSpec((tile, features), lambda i, owners: (i, 0)),
            pl.BlockSpec((tile, outputs), lambda i, owners: (i, 0)),
        ],
        out_specs=pl.BlockSpec((tile, 2 * rank_width), lambda i, owners: (i, 0)),
        scratch_shapes=[
            pltpu.VMEM((count, rank_width, width), jnp.bfloat16),
            pltpu.VMEM((rank_width, features), jnp.bfloat16),
            pltpu.VMEM((rank_width, outputs), jnp.bfloat16),
        ],
    )
    return pl.pallas_call(
        projection_kernel(count, features // count, outputs // count, rank_width),
        grid_spec=grid_spec,
        out_shape=jax.ShapeDtypeStruct((local_tokens, 2 * rank_width), jnp.bfloat16),
        compiler_params=pltpu.CompilerParams(dimension_semantics=("arbitrary",)),
    )(owners, *blocks, hidden, out_grad)


def local(hidden, out_grad, hidden_basis, output_basis, owner_ids, doc_slot):
    devices = lax.axis_size("dp")
    local_tokens = hidden.shape[0]
    capacity = 2 * local_tokens // devices
    rank_width = hidden_basis.shape[0]
    buffer_len = devices * capacity
    blocks, owners = ring_gather(jnp.concatenate([hidden_basis, output_basis], axis=1), devices)
    rows = project_rows(blocks, owners, hidden, out_grad)
    targets = owner_ids[:, 0]
    member = (targets[:, None] == jnp.arange(devices, dtype=jnp.int32)[None, :]).astype(jnp.bfloat16)
    token_ids = jnp.arange(local_tokens, dtype=jnp.int32)
    earlier = (token_ids[:, None] > token_ids[None, :]).astype(jnp.bfloat16)
    before = lax.dot_general(
        earlier, member, (((1,), (0,)), ((), ())), preferred_element_type=jnp.float32
    )
    position = jnp.sum(member.astype(jnp.float32) * before, axis=1).astype(jnp.int32)
    slot_index = targets * capacity + position
    dispatch = (
        jnp.arange(buffer_len, dtype=jnp.int32)[:, None] == slot_index[None, :]
    ).astype(jnp.bfloat16)
    buffer = lax.dot_general(
        dispatch, rows, (((1,), (0,)), ((), ())), preferred_element_type=jnp.float32
    ).astype(jnp.bfloat16)
    label = lax.dot_general(
        dispatch, (doc_slot + 1).astype(jnp.bfloat16), (((1,), (0,)), ((), ())),
        preferred_element_type=jnp.float32,
    ).astype(jnp.bfloat16)
    width = 2 * rank_width
    label_row = jnp.pad(label.reshape(devices, 1, capacity), ((0, 0), (0, 0), (0, width - capacity)))
    packed = jnp.concatenate([buffer.reshape(devices, capacity, width), label_row], axis=1)
    arrived = lax.all_to_all(packed, "dp", 0, 0, tiled=True)
    rows_in = arrived[:, :capacity, :].reshape(buffer_len, width)
    label_in = arrived[:, capacity, :capacity].reshape(buffer_len, 1)
    left_in = rows_in[:, :rank_width]
    right_in = rows_in[:, rank_width:]
    wanted = (jnp.arange(DOCS_DEV, dtype=jnp.int32) + 1).astype(jnp.bfloat16)[None, :]
    selector = (label_in == wanted).astype(jnp.bfloat16)
    weighted = (selector[:, :, None] * left_in[:, None, :]).reshape(buffer_len, DOCS_DEV * rank_width)
    grads = lax.dot_general(
        weighted, right_in, (((0,), (0,)), ((), ())), preferred_element_type=jnp.float32
    )
    return grads.reshape(DOCS_DEV, rank_width * rank_width)


def solution(mesh):
    placed = (
        P(("groups", "dp"), None),
        P(("groups", "dp"), None),
        P(None, "dp"),
        P(None, "dp"),
        P(("groups", "dp"), None),
        P(("groups", "dp")),
    )
    return jax.shard_map(
        local, mesh=mesh, in_specs=placed, out_specs=P(("groups", "dp"), None), check_vma=False
    )
```

```python
import numpy as np
import jax
import jax.numpy as jnp
from jax import lax
from jax.experimental import pallas as pl
from jax.experimental.pallas import tpu as pltpu
from jax.sharding import PartitionSpec as P

DOCS_DEV = 8


def ring_planes(devices):
    chips = devices // 2
    if devices % 2 or chips < 2:
        return [list(range(devices))]
    if chips % 2 == 0 and chips >= 4:
        order = list(range(0, chips, 2)) + list(range(chips - 1, 0, -2))
    else:
        order = list(range(chips))
    return [[2 * chip + core for chip in order] for core in range(2)]


def ring_gather(block, devices):
    planes = ring_planes(devices)
    length = len(planes[0])
    me = lax.axis_index("dp")
    place = np.zeros(devices, np.int32)
    plane_of = np.zeros(devices, np.int32)
    for plane, members in enumerate(planes):
        for spot, member in enumerate(members):
            place[member] = spot
            plane_of[member] = plane
    spot = jnp.asarray(place)[me]
    plane = jnp.asarray(plane_of)[me]
    forward = [(ring[t], ring[(t + 1) % length]) for ring in planes for t in range(length)]
    backward = [(ring[t], ring[(t - 1) % length]) for ring in planes for t in range(length)]
    blocks = [block]
    shifts = [0]
    moving = block
    for step in range(1, length // 2 + 1):
        moving = lax.ppermute(moving, "dp", forward)
        blocks.append(moving)
        shifts.append(-step)
    moving = block
    for step in range(1, length - length // 2):
        moving = lax.ppermute(moving, "dp", backward)
        blocks.append(moving)
        shifts.append(step)
    spots = (spot + jnp.asarray(np.array(shifts, np.int32))) % length
    chips = jnp.asarray(np.array(planes[0], np.int32) // len(planes))
    hit = spots[:, None] == jnp.arange(length, dtype=jnp.int32)[None, :]
    chip_of = jnp.sum(jnp.where(hit, chips[None, :], 0), axis=1)
    if len(planes) == 1:
        return blocks, None, chip_of.astype(jnp.int32)
    mine = jnp.stack(blocks)
    swap = list(zip(planes[0], planes[1])) + list(zip(planes[1], planes[0]))
    other = lax.ppermute(mine, "dp", swap)
    owners = jnp.concatenate([chip_of * 2 + plane, chip_of * 2 + 1 - plane])
    return blocks, other, owners.astype(jnp.int32)


def projection_kernel(count, devices, hidden_cols, output_cols, rank_width, paired):
    def kernel(owners, *refs):
        blocks = refs[:count]
        rest = refs[count:]
        if paired:
            other_ref, rest = rest[0], rest[1:]
        hidden_ref, grad_ref, rows_ref, stacked, hidden_full, output_full = rest

        @pl.when(pl.program_id(0) == 0)
        def _():
            for k in range(count):
                stacked[owners[k]] = blocks[k][...]
                if paired:
                    stacked[owners[count + k]] = other_ref[k]
            for d in range(devices):
                hidden_full[:, d * hidden_cols:(d + 1) * hidden_cols] = stacked[d, :, :hidden_cols]
                output_full[:, d * output_cols:(d + 1) * output_cols] = stacked[d, :, hidden_cols:]

        dims = (((1,), (1,)), ((), ()))
        left = lax.dot_general(hidden_ref[...], hidden_full[...], dims, preferred_element_type=jnp.float32)
        right = lax.dot_general(grad_ref[...], output_full[...], dims, preferred_element_type=jnp.float32)
        rows_ref[:, :rank_width] = left.astype(jnp.bfloat16)
        rows_ref[:, rank_width:] = right.astype(jnp.bfloat16)

    return kernel


def project_rows(blocks, other, owners, hidden, out_grad, devices):
    count = len(blocks)
    paired = other is not None
    rank_width, width = blocks[0].shape
    local_tokens, features = hidden.shape
    outputs = out_grad.shape[1]
    tile = 128 if local_tokens % 128 == 0 else local_tokens
    whole = pl.BlockSpec((rank_width, width), lambda i, owners: (0, 0))
    grid_spec = pltpu.PrefetchScalarGridSpec(
        num_scalar_prefetch=1,
        grid=(local_tokens // tile,),
        in_specs=[whole] * count + [pl.BlockSpec((count, rank_width, width), lambda i, owners: (0, 0, 0))] * paired + [
            pl.BlockSpec((tile, features), lambda i, owners: (i, 0)),
            pl.BlockSpec((tile, outputs), lambda i, owners: (i, 0)),
        ],
        out_specs=pl.BlockSpec((tile, 2 * rank_width), lambda i, owners: (i, 0)),
        scratch_shapes=[
            pltpu.VMEM((devices, rank_width, width), jnp.bfloat16),
            pltpu.VMEM((rank_width, features), jnp.bfloat16),
            pltpu.VMEM((rank_width, outputs), jnp.bfloat16),
        ],
    )
    return pl.pallas_call(
        projection_kernel(count, devices, features // devices, outputs // devices, rank_width, paired),
        grid_spec=grid_spec,
        out_shape=jax.ShapeDtypeStruct((local_tokens, 2 * rank_width), jnp.bfloat16),
        compiler_params=pltpu.CompilerParams(dimension_semantics=("arbitrary",)),
    )(owners, *blocks, *([other] if paired else []), hidden, out_grad)


def local(hidden, out_grad, hidden_basis, output_basis, owner_ids, doc_slot):
    devices = lax.axis_size("dp")
    local_tokens = hidden.shape[0]
    capacity = 2 * local_tokens // devices
    rank_width = hidden_basis.shape[0]
    buffer_len = devices * capacity
    blocks, other, owners = ring_gather(jnp.concatenate([hidden_basis, output_basis], axis=1), devices)
    rows = project_rows(blocks, other, owners, hidden, out_grad, devices)
    targets = owner_ids[:, 0]
    member = (targets[:, None] == jnp.arange(devices, dtype=jnp.int32)[None, :]).astype(jnp.bfloat16)
    token_ids = jnp.arange(local_tokens, dtype=jnp.int32)
    earlier = (token_ids[:, None] > token_ids[None, :]).astype(jnp.bfloat16)
    before = lax.dot_general(
        earlier, member, (((1,), (0,)), ((), ())), preferred_element_type=jnp.float32
    )
    position = jnp.sum(member.astype(jnp.float32) * before, axis=1).astype(jnp.int32)
    slot_index = targets * capacity + position
    dispatch = (
        jnp.arange(buffer_len, dtype=jnp.int32)[:, None] == slot_index[None, :]
    ).astype(jnp.bfloat16)
    buffer = lax.dot_general(
        dispatch, rows, (((1,), (0,)), ((), ())), preferred_element_type=jnp.float32
    ).astype(jnp.bfloat16)
    label = lax.dot_general(
        dispatch, (doc_slot + 1).astype(jnp.bfloat16), (((1,), (0,)), ((), ())),
        preferred_element_type=jnp.float32,
    ).astype(jnp.bfloat16)
    width = 2 * rank_width
    label_row = jnp.pad(label.reshape(devices, 1, capacity), ((0, 0), (0, 0), (0, width - capacity)))
    packed = jnp.concatenate([buffer.reshape(devices, capacity, width), label_row], axis=1)
    arrived = lax.all_to_all(packed, "dp", 0, 0, tiled=True)
    rows_in = arrived[:, :capacity, :].reshape(buffer_len, width)
    label_in = arrived[:, capacity, :capacity].reshape(buffer_len, 1)
    left_in = rows_in[:, :rank_width]
    right_in = rows_in[:, rank_width:]
    wanted = (jnp.arange(DOCS_DEV, dtype=jnp.int32) + 1).astype(jnp.bfloat16)[None, :]
    selector = (label_in == wanted).astype(jnp.bfloat16)
    weighted = (selector[:, :, None] * left_in[:, None, :]).reshape(buffer_len, DOCS_DEV * rank_width)
    grads = lax.dot_general(
        weighted, right_in, (((0,), (0,)), ((), ())), preferred_element_type=jnp.float32
    )
    return grads.reshape(DOCS_DEV, rank_width * rank_width)


def solution(mesh):
    placed = (
        P(("groups", "dp"), None),
        P(("groups", "dp"), None),
        P(None, "dp"),
        P(None, "dp"),
        P(("groups", "dp"), None),
        P(("groups", "dp")),
    )
    return jax.shard_map(
        local, mesh=mesh, in_specs=placed, out_specs=P(("groups", "dp"), None), check_vma=False
    )
```

```python
import numpy as np
import jax
import jax.numpy as jnp
from jax import lax
from jax.sharding import PartitionSpec as P

DOCS_DEV = 8


def ring_planes(devices):
    chips = devices // 2
    if devices % 2 or chips < 2:
        return [list(range(devices))]
    if chips % 2 == 0 and chips >= 4:
        order = list(range(0, chips, 2)) + list(range(chips - 1, 0, -2))
    else:
        order = list(range(chips))
    return [[2 * chip + core for chip in order] for core in range(2)]


def ring_gather(block, devices):
    planes = ring_planes(devices)
    length = len(planes[0])
    me = lax.axis_index("dp")
    place = np.zeros(devices, np.int32)
    plane_of = np.zeros(devices, np.int32)
    for plane, members in enumerate(planes):
        for spot, member in enumerate(members):
            place[member] = spot
            plane_of[member] = plane
    spot = jnp.asarray(place)[me]
    plane = jnp.asarray(plane_of)[me]
    forward = [(ring[t], ring[(t + 1) % length]) for ring in planes for t in range(length)]
    backward = [(ring[t], ring[(t - 1) % length]) for ring in planes for t in range(length)]
    blocks = [block]
    shifts = [0]
    moving = block
    for step in range(1, length // 2 + 1):
        moving = lax.ppermute(moving, "dp", forward)
        blocks.append(moving)
        shifts.append(-step)
    moving = block
    for step in range(1, length - length // 2):
        moving = lax.ppermute(moving, "dp", backward)
        blocks.append(moving)
        shifts.append(step)
    spots = (spot + jnp.asarray(np.array(shifts, np.int32))) % length
    chips = jnp.asarray(np.array(planes[0], np.int32) // len(planes))
    hit = spots[:, None] == jnp.arange(length, dtype=jnp.int32)[None, :]
    chip_of = jnp.sum(jnp.where(hit, chips[None, :], 0), axis=1)
    if len(planes) == 1:
        return blocks, None, chip_of.astype(jnp.int32)
    mine = jnp.stack(blocks)
    swap = list(zip(planes[0], planes[1])) + list(zip(planes[1], planes[0]))
    other = lax.ppermute(mine, "dp", swap)
    owners = jnp.concatenate([chip_of * 2 + plane, chip_of * 2 + 1 - plane])
    return blocks, other, owners.astype(jnp.int32)


def partial_rows(hidden_parts, grad_parts, block, owner, hidden_cols):
    dims = (((1,), (1,)), ((), ()))
    left = lax.dot_general(hidden_parts[owner], block[:, :hidden_cols], dims, preferred_element_type=jnp.float32)
    right = lax.dot_general(grad_parts[owner], block[:, hidden_cols:], dims, preferred_element_type=jnp.float32)
    return left, right


def project_rows(blocks, other, owners, hidden, out_grad, devices):
    local_tokens, features = hidden.shape
    hidden_cols = features // devices
    output_cols = out_grad.shape[1] // devices
    hidden_parts = hidden.reshape(local_tokens, devices, hidden_cols).transpose(1, 0, 2)
    grad_parts = out_grad.reshape(local_tokens, devices, output_cols).transpose(1, 0, 2)
    pieces = list(blocks)
    if other is not None:
        pieces = pieces + [other[k] for k in range(len(blocks))]
    left = None
    right = None
    for k, block in enumerate(pieces):
        part_left, part_right = partial_rows(hidden_parts, grad_parts, block, owners[k], hidden_cols)
        left = part_left if left is None else left + part_left
        right = part_right if right is None else right + part_right
    return jnp.concatenate([left, right], axis=1).astype(jnp.bfloat16)


def local(hidden, out_grad, hidden_basis, output_basis, owner_ids, doc_slot):
    devices = lax.axis_size("dp")
    local_tokens = hidden.shape[0]
    capacity = 2 * local_tokens // devices
    rank_width = hidden_basis.shape[0]
    buffer_len = devices * capacity
    blocks, other, owners = ring_gather(jnp.concatenate([hidden_basis, output_basis], axis=1), devices)
    rows = project_rows(blocks, other, owners, hidden, out_grad, devices)
    targets = owner_ids[:, 0]
    member = (targets[:, None] == jnp.arange(devices, dtype=jnp.int32)[None, :]).astype(jnp.bfloat16)
    token_ids = jnp.arange(local_tokens, dtype=jnp.int32)
    earlier = (token_ids[:, None] > token_ids[None, :]).astype(jnp.bfloat16)
    before = lax.dot_general(
        earlier, member, (((1,), (0,)), ((), ())), preferred_element_type=jnp.float32
    )
    position = jnp.sum(member.astype(jnp.float32) * before, axis=1).astype(jnp.int32)
    slot_index = targets * capacity + position
    dispatch = (
        jnp.arange(buffer_len, dtype=jnp.int32)[:, None] == slot_index[None, :]
    ).astype(jnp.bfloat16)
    buffer = lax.dot_general(
        dispatch, rows, (((1,), (0,)), ((), ())), preferred_element_type=jnp.float32
    ).astype(jnp.bfloat16)
    label = lax.dot_general(
        dispatch, (doc_slot + 1).astype(jnp.bfloat16), (((1,), (0,)), ((), ())),
        preferred_element_type=jnp.float32,
    ).astype(jnp.bfloat16)
    width = 2 * rank_width
    label_row = jnp.pad(label.reshape(devices, 1, capacity), ((0, 0), (0, 0), (0, width - capacity)))
    packed = jnp.concatenate([buffer.reshape(devices, capacity, width), label_row], axis=1)
    arrived = lax.all_to_all(packed, "dp", 0, 0, tiled=True)
    rows_in = arrived[:, :capacity, :].reshape(buffer_len, width)
    label_in = arrived[:, capacity, :capacity].reshape(buffer_len, 1)
    left_in = rows_in[:, :rank_width]
    right_in = rows_in[:, rank_width:]
    wanted = (jnp.arange(DOCS_DEV, dtype=jnp.int32) + 1).astype(jnp.bfloat16)[None, :]
    selector = (label_in == wanted).astype(jnp.bfloat16)
    weighted = (selector[:, :, None] * left_in[:, None, :]).reshape(buffer_len, DOCS_DEV * rank_width)
    grads = lax.dot_general(
        weighted, right_in, (((0,), (0,)), ((), ())), preferred_element_type=jnp.float32
    )
    return grads.reshape(DOCS_DEV, rank_width * rank_width)


def solution(mesh):
    placed = (
        P(("groups", "dp"), None),
        P(("groups", "dp"), None),
        P(None, "dp"),
        P(None, "dp"),
        P(("groups", "dp"), None),
        P(("groups", "dp")),
    )
    return jax.shard_map(
        local, mesh=mesh, in_specs=placed, out_specs=P(("groups", "dp"), None), check_vma=False
    )
```

```python
import numpy as np
import jax
import jax.numpy as jnp
from jax import lax
from jax.experimental import pallas as pl
from jax.experimental.pallas import tpu as pltpu
from jax.sharding import PartitionSpec as P

DOCS_DEV = 8


def ring_planes(devices):
    chips = devices // 2
    if devices % 2 or chips < 2:
        return [list(range(devices))]
    if chips % 2 == 0 and chips >= 4:
        order = list(range(0, chips, 2)) + list(range(chips - 1, 0, -2))
    else:
        order = list(range(chips))
    return [[2 * chip + core for chip in order] for core in range(2)]


def ring_gather(block, devices):
    planes = ring_planes(devices)
    length = len(planes[0])
    me = lax.axis_index("dp")
    place = np.zeros(devices, np.int32)
    plane_of = np.zeros(devices, np.int32)
    for plane, members in enumerate(planes):
        for spot, member in enumerate(members):
            place[member] = spot
            plane_of[member] = plane
    forward = [(ring[t], ring[(t + 1) % length]) for ring in planes for t in range(length)]
    backward = [(ring[t], ring[(t - 1) % length]) for ring in planes for t in range(length)]
    blocks = [block]
    shifts = [0]
    moving = block
    for step in range(1, length // 2 + 1):
        moving = lax.ppermute(moving, "dp", forward)
        blocks.append(moving)
        shifts.append(-step)
    moving = block
    for step in range(1, length - length // 2):
        moving = lax.ppermute(moving, "dp", backward)
        blocks.append(moving)
        shifts.append(step)
    table = np.zeros((devices, len(shifts) * len(planes)), np.int32)
    for member in range(devices):
        for k, shift in enumerate(shifts):
            for side in range(len(planes)):
                ring = planes[(plane_of[member] + side) % len(planes)]
                table[member, side * len(shifts) + k] = ring[(place[member] + shift) % length]
    owners = jnp.asarray(table)[me]
    if len(planes) == 1:
        return blocks, None, owners
    mine = jnp.stack(blocks)
    swap = list(zip(planes[0], planes[1])) + list(zip(planes[1], planes[0]))
    other = lax.ppermute(mine, "dp", swap)
    return blocks, other, owners


def projection_kernel(count, devices, hidden_cols, output_cols, rank_width, paired):
    def kernel(owners, *refs):
        blocks = refs[:count]
        rest = refs[count:]
        if paired:
            other_ref, rest = rest[0], rest[1:]
        hidden_ref, grad_ref, dispatch_ref, buffer_ref, rows, stacked, hidden_full, output_full = rest
        step = pl.program_id(0)
        tile = hidden_ref.shape[0]

        @pl.when(pl.program_id(0) == 0)
        def _():
            for k in range(count):
                stacked[owners[k]] = blocks[k][...]
                if paired:
                    stacked[owners[count + k]] = other_ref[k]
            for d in range(devices):
                hidden_full[:, d * hidden_cols:(d + 1) * hidden_cols] = stacked[d, :, :hidden_cols]
                output_full[:, d * output_cols:(d + 1) * output_cols] = stacked[d, :, hidden_cols:]

        dims = (((1,), (1,)), ((), ()))
        left = lax.dot_general(hidden_ref[...], hidden_full[...], dims, preferred_element_type=jnp.float32)
        right = lax.dot_general(grad_ref[...], output_full[...], dims, preferred_element_type=jnp.float32)
        at = pl.multiple_of(step * tile, tile)
        rows[pl.ds(at, tile), :rank_width] = left.astype(jnp.bfloat16)
        rows[pl.ds(at, tile), rank_width:] = right.astype(jnp.bfloat16)

        @pl.when(step == pl.num_programs(0) - 1)
        def _():
            placed = lax.dot_general(
                dispatch_ref[...], rows[...], (((1,), (0,)), ((), ())), preferred_element_type=jnp.float32
            )
            buffer_ref[...] = placed.astype(jnp.bfloat16)

    return kernel


def project_rows(blocks, other, owners, hidden, out_grad, dispatch, devices):
    count = len(blocks)
    paired = other is not None
    rank_width, width = blocks[0].shape
    local_tokens, features = hidden.shape
    outputs = out_grad.shape[1]
    tile = 128 if local_tokens % 128 == 0 else local_tokens
    whole = pl.BlockSpec((rank_width, width), lambda i, owners: (0, 0))
    grid_spec = pltpu.PrefetchScalarGridSpec(
        num_scalar_prefetch=1,
        grid=(local_tokens // tile,),
        in_specs=[whole] * count + [pl.BlockSpec((count, rank_width, width), lambda i, owners: (0, 0, 0))] * paired + [
            pl.BlockSpec((tile, features), lambda i, owners: (i, 0)),
            pl.BlockSpec((tile, outputs), lambda i, owners: (i, 0)),
            pl.BlockSpec(dispatch.shape, lambda i, owners: (0, 0)),
        ],
        out_specs=pl.BlockSpec((dispatch.shape[0], 2 * rank_width), lambda i, owners: (0, 0)),
        scratch_shapes=[
            pltpu.VMEM((local_tokens, 2 * rank_width), jnp.bfloat16),
            pltpu.VMEM((devices, rank_width, width), jnp.bfloat16),
            pltpu.VMEM((rank_width, features), jnp.bfloat16),
            pltpu.VMEM((rank_width, outputs), jnp.bfloat16),
        ],
    )
    return pl.pallas_call(
        projection_kernel(count, devices, features // devices, outputs // devices, rank_width, paired),
        grid_spec=grid_spec,
        out_shape=jax.ShapeDtypeStruct((dispatch.shape[0], 2 * rank_width), jnp.bfloat16),
        compiler_params=pltpu.CompilerParams(dimension_semantics=("arbitrary",)),
    )(owners, *blocks, *([other] if paired else []), hidden, out_grad, dispatch)


def local(hidden, out_grad, hidden_basis, output_basis, owner_ids, doc_slot):
    devices = lax.axis_size("dp")
    local_tokens = hidden.shape[0]
    capacity = 2 * local_tokens // devices
    rank_width = hidden_basis.shape[0]
    buffer_len = devices * capacity
    blocks, other, owners = ring_gather(jnp.concatenate([hidden_basis, output_basis], axis=1), devices)
    targets = owner_ids[:, 0]
    member = (targets[:, None] == jnp.arange(devices, dtype=jnp.int32)[None, :]).astype(jnp.bfloat16)
    token_ids = jnp.arange(local_tokens, dtype=jnp.int32)
    earlier = (token_ids[:, None] > token_ids[None, :]).astype(jnp.bfloat16)
    before = lax.dot_general(
        earlier, member, (((1,), (0,)), ((), ())), preferred_element_type=jnp.float32
    )
    position = jnp.sum(member.astype(jnp.float32) * before, axis=1).astype(jnp.int32)
    slot_index = targets * capacity + position
    dispatch = (
        jnp.arange(buffer_len, dtype=jnp.int32)[:, None] == slot_index[None, :]
    ).astype(jnp.bfloat16)
    buffer = project_rows(blocks, other, owners, hidden, out_grad, dispatch, devices)
    label = lax.dot_general(
        dispatch, (doc_slot + 1).astype(jnp.bfloat16), (((1,), (0,)), ((), ())),
        preferred_element_type=jnp.float32,
    ).astype(jnp.bfloat16)
    width = 2 * rank_width
    label_row = jnp.pad(label.reshape(devices, 1, capacity), ((0, 0), (0, 0), (0, width - capacity)))
    packed = jnp.concatenate([buffer.reshape(devices, capacity, width), label_row], axis=1)
    arrived = lax.all_to_all(packed, "dp", 0, 0, tiled=True)
    rows_in = arrived[:, :capacity, :].reshape(buffer_len, width)
    label_in = arrived[:, capacity, :capacity].reshape(buffer_len, 1)
    left_in = rows_in[:, :rank_width]
    right_in = rows_in[:, rank_width:]
    wanted = (jnp.arange(DOCS_DEV, dtype=jnp.int32) + 1).astype(jnp.bfloat16)[None, :]
    selector = (label_in == wanted).astype(jnp.bfloat16)
    weighted = (selector[:, :, None] * left_in[:, None, :]).reshape(buffer_len, DOCS_DEV * rank_width)
    grads = lax.dot_general(
        weighted, right_in, (((0,), (0,)), ((), ())), preferred_element_type=jnp.float32
    )
    return grads.reshape(DOCS_DEV, rank_width * rank_width)


def solution(mesh):
    placed = (
        P(("groups", "dp"), None),
        P(("groups", "dp"), None),
        P(None, "dp"),
        P(None, "dp"),
        P(("groups", "dp"), None),
        P(("groups", "dp")),
    )
    return jax.shard_map(
        local, mesh=mesh, in_specs=placed, out_specs=P(("groups", "dp"), None), check_vma=False
    )
```

```python
import numpy as np
import jax
import jax.numpy as jnp
from jax import lax
from jax.experimental import pallas as pl
from jax.experimental.pallas import tpu as pltpu
from jax.sharding import PartitionSpec as P

DOCS_DEV = 8


def ring_planes(devices):
    chips = devices // 2
    if devices % 2 or chips < 2:
        return [list(range(devices))]
    if chips % 2 == 0 and chips >= 4:
        order = list(range(0, chips, 2)) + list(range(chips - 1, 0, -2))
    else:
        order = list(range(chips))
    return [[2 * chip + core for chip in order] for core in range(2)]


def ring_gather(block, devices):
    planes = ring_planes(devices)
    length = len(planes[0])
    place = np.zeros(devices, np.int32)
    plane_of = np.zeros(devices, np.int32)
    for plane, members in enumerate(planes):
        for spot, member in enumerate(members):
            place[member] = spot
            plane_of[member] = plane
    forward = [(ring[t], ring[(t + 1) % length]) for ring in planes for t in range(length)]
    backward = [(ring[t], ring[(t - 1) % length]) for ring in planes for t in range(length)]
    blocks = [block]
    shifts = [0]
    moving = block
    for step in range(1, length // 2 + 1):
        moving = lax.ppermute(moving, "dp", forward)
        blocks.append(moving)
        shifts.append(-step)
    moving = block
    for step in range(1, length - length // 2):
        moving = lax.ppermute(moving, "dp", backward)
        blocks.append(moving)
        shifts.append(step)
    table = np.zeros((devices, len(shifts) * len(planes)), np.int32)
    for member in range(devices):
        for k, shift in enumerate(shifts):
            for side in range(len(planes)):
                ring = planes[(plane_of[member] + side) % len(planes)]
                table[member, side * len(shifts) + k] = ring[(place[member] + shift) % length]
    owners = jnp.asarray(table.reshape(-1))
    if len(planes) == 1:
        return blocks, None, owners
    mine = jnp.stack(blocks)
    swap = list(zip(planes[0], planes[1])) + list(zip(planes[1], planes[0]))
    other = lax.ppermute(mine, "dp", swap)
    return blocks, other, owners


def projection_kernel(count, devices, hidden_cols, output_cols, rank_width, paired, capacity):
    width = count * (2 if paired else 1)

    def kernel(table, *refs):
        blocks = refs[:count]
        rest = refs[count:]
        if paired:
            other_ref, rest = rest[0], rest[1:]
        hidden_ref, grad_ref, owner_ref, slot_ref, out_ref, rows, stacked, hidden_full, output_full = rest
        step = pl.program_id(0)
        tile = hidden_ref.shape[0]
        me = lax.axis_index("dp")

        @pl.when(step == 0)
        def _():
            for k in range(count):
                stacked[table[me * width + k]] = blocks[k][...]
                if paired:
                    stacked[table[me * width + count + k]] = other_ref[k]
            for d in range(devices):
                hidden_full[:, d * hidden_cols:(d + 1) * hidden_cols] = stacked[d, :, :hidden_cols]
                output_full[:, d * output_cols:(d + 1) * output_cols] = stacked[d, :, hidden_cols:]

        dims = (((1,), (1,)), ((), ()))
        left = lax.dot_general(hidden_ref[...], hidden_full[...], dims, preferred_element_type=jnp.float32)
        right = lax.dot_general(grad_ref[...], output_full[...], dims, preferred_element_type=jnp.float32)
        at = pl.multiple_of(step * tile, tile)
        rows[pl.ds(at, tile), :rank_width] = left.astype(jnp.bfloat16)
        rows[pl.ds(at, tile), rank_width:] = right.astype(jnp.bfloat16)

        @pl.when(step == pl.num_programs(0) - 1)
        def _():
            tokens, lanes = rows.shape
            targets = owner_ref[...]
            member = (targets == lax.broadcasted_iota(jnp.int32, (tokens, devices), 1)).astype(jnp.bfloat16)
            earlier = (
                lax.broadcasted_iota(jnp.int32, (tokens, tokens), 0)
                > lax.broadcasted_iota(jnp.int32, (tokens, tokens), 1)
            ).astype(jnp.bfloat16)
            before = jnp.dot(earlier, member, preferred_element_type=jnp.float32)
            position = jnp.sum(member.astype(jnp.float32) * before, axis=1, keepdims=True).astype(jnp.int32)
            slot_index = targets * capacity + position
            spread = (
                slot_index == lax.broadcasted_iota(jnp.int32, (tokens, devices * capacity), 1)
            ).astype(jnp.bfloat16)
            down = (((0,), (0,)), ((), ()))
            placed = lax.dot_general(spread, rows[...], down, preferred_element_type=jnp.float32)
            placed = placed.astype(jnp.bfloat16)
            slots = jnp.broadcast_to(slot_ref[...].astype(jnp.float32), (8, tokens)).T[:, :1]
            tagged = member * (slots + 1.0).astype(jnp.bfloat16)
            spot = (position == lax.broadcasted_iota(jnp.int32, (tokens, lanes), 1)).astype(jnp.bfloat16)
            labels = lax.dot_general(tagged, spot, down, preferred_element_type=jnp.float32)
            labels = labels.astype(jnp.bfloat16)
            for d in range(devices):
                out_ref[d, :capacity, :] = placed[d * capacity:(d + 1) * capacity, :]
                out_ref[d, capacity:, :] = labels[d:d + 1, :]

    return kernel


def project_rows(blocks, other, table, hidden, out_grad, owner_ids, doc_slot, devices, capacity):
    count = len(blocks)
    paired = other is not None
    rank_width, width = blocks[0].shape
    local_tokens, features = hidden.shape
    outputs = out_grad.shape[1]
    tile = 128 if local_tokens % 128 == 0 else local_tokens
    whole = pl.BlockSpec((rank_width, width), lambda i, table: (0, 0))
    grid_spec = pltpu.PrefetchScalarGridSpec(
        num_scalar_prefetch=1,
        grid=(local_tokens // tile,),
        in_specs=[whole] * count + [pl.BlockSpec((count, rank_width, width), lambda i, table: (0, 0, 0))] * paired + [
            pl.BlockSpec((tile, features), lambda i, table: (i, 0)),
            pl.BlockSpec((tile, outputs), lambda i, table: (i, 0)),
            pl.BlockSpec((local_tokens, 1), lambda i, table: (0, 0)),
            pl.BlockSpec((1, local_tokens), lambda i, table: (0, 0)),
        ],
        out_specs=pl.BlockSpec((devices, capacity + 1, 2 * rank_width), lambda i, table: (0, 0, 0)),
        scratch_shapes=[
            pltpu.VMEM((local_tokens, 2 * rank_width), jnp.bfloat16),
            pltpu.VMEM((devices, rank_width, width), jnp.bfloat16),
            pltpu.VMEM((rank_width, features), jnp.bfloat16),
            pltpu.VMEM((rank_width, outputs), jnp.bfloat16),
        ],
    )
    return pl.pallas_call(
        projection_kernel(count, devices, features // devices, outputs // devices, rank_width, paired, capacity),
        grid_spec=grid_spec,
        out_shape=jax.ShapeDtypeStruct((devices, capacity + 1, 2 * rank_width), jnp.bfloat16),
        compiler_params=pltpu.CompilerParams(dimension_semantics=("arbitrary",)),
    )(table, *blocks, *([other] if paired else []), hidden, out_grad, owner_ids, doc_slot.reshape(1, -1))


def local(hidden, out_grad, hidden_basis, output_basis, owner_ids, doc_slot):
    devices = lax.axis_size("dp")
    local_tokens = hidden.shape[0]
    capacity = 2 * local_tokens // devices
    rank_width = hidden_basis.shape[0]
    buffer_len = devices * capacity
    blocks, other, table = ring_gather(jnp.concatenate([hidden_basis, output_basis], axis=1), devices)
    packed = project_rows(blocks, other, table, hidden, out_grad, owner_ids, doc_slot, devices, capacity)
    arrived = lax.all_to_all(packed, "dp", 0, 0, tiled=True)
    rows_in = arrived[:, :capacity, :].reshape(buffer_len, 2 * rank_width)
    label_in = arrived[:, capacity, :capacity].reshape(buffer_len, 1)
    left_in = rows_in[:, :rank_width]
    right_in = rows_in[:, rank_width:]
    wanted = (jnp.arange(DOCS_DEV, dtype=jnp.int32) + 1).astype(jnp.bfloat16)[None, :]
    selector = (label_in == wanted).astype(jnp.bfloat16)
    weighted = (selector[:, :, None] * left_in[:, None, :]).reshape(buffer_len, DOCS_DEV * rank_width)
    grads = lax.dot_general(
        weighted, right_in, (((0,), (0,)), ((), ())), preferred_element_type=jnp.float32
    )
    return grads.reshape(DOCS_DEV, rank_width * rank_width)


def solution(mesh):
    placed = (
        P(("groups", "dp"), None),
        P(("groups", "dp"), None),
        P(None, "dp"),
        P(None, "dp"),
        P(("groups", "dp"), None),
        P(("groups", "dp")),
    )
    return jax.shard_map(
        local, mesh=mesh, in_specs=placed, out_specs=P(("groups", "dp"), None), check_vma=False
    )
```

```python
import numpy as np
import jax
import jax.numpy as jnp
from jax import lax
from jax.experimental import pallas as pl
from jax.experimental.pallas import tpu as pltpu
from jax.sharding import PartitionSpec as P

DOCS_DEV = 8


def ring_planes(devices):
    chips = devices // 2
    if devices % 2 or chips < 2:
        return [list(range(devices))]
    if chips % 2 == 0 and chips >= 4:
        order = list(range(0, chips, 2)) + list(range(chips - 1, 0, -2))
    else:
        order = list(range(chips))
    return [[2 * chip + core for chip in order] for core in range(2)]


def ring_gather(block, devices):
    planes = ring_planes(devices)
    length = len(planes[0])
    place = np.zeros(devices, np.int32)
    plane_of = np.zeros(devices, np.int32)
    for plane, members in enumerate(planes):
        for spot, member in enumerate(members):
            place[member] = spot
            plane_of[member] = plane
    forward = [(ring[t], ring[(t + 1) % length]) for ring in planes for t in range(length)]
    backward = [(ring[t], ring[(t - 1) % length]) for ring in planes for t in range(length)]
    blocks = [block]
    shifts = [0]
    moving = block
    for step in range(1, length // 2 + 1):
        moving = lax.ppermute(moving, "dp", forward)
        blocks.append(moving)
        shifts.append(-step)
    moving = block
    for step in range(1, length - length // 2):
        moving = lax.ppermute(moving, "dp", backward)
        blocks.append(moving)
        shifts.append(step)
    table = np.zeros((devices, len(shifts) * len(planes)), np.int32)
    for member in range(devices):
        for k, shift in enumerate(shifts):
            for side in range(len(planes)):
                ring = planes[(plane_of[member] + side) % len(planes)]
                table[member, side * len(shifts) + k] = ring[(place[member] + shift) % length]
    owners = jnp.asarray(table.reshape(-1))
    if len(planes) == 1:
        return blocks, None, owners
    mine = jnp.stack(blocks)
    swap = list(zip(planes[0], planes[1])) + list(zip(planes[1], planes[0]))
    other = lax.ppermute(mine, "dp", swap)
    return blocks, other, owners


def projection_kernel(count, devices, hidden_cols, output_cols, rank_width, paired, capacity):
    width = count * (2 if paired else 1)

    def kernel(table, *refs):
        blocks = refs[:count]
        rest = refs[count:]
        if paired:
            other_ref, rest = rest[0], rest[1:]
        hidden_ref, grad_ref, owner_ref, slot_ref, out_ref, rows, stacked, hidden_full, output_full = rest
        step = pl.program_id(0)
        tile = hidden_ref.shape[0]
        me = lax.axis_index("dp")

        @pl.when(step == 0)
        def _():
            for k in range(count):
                stacked[table[me * width + k]] = blocks[k][...]
                if paired:
                    stacked[table[me * width + count + k]] = other_ref[k]
            for d in range(devices):
                hidden_full[:, d * hidden_cols:(d + 1) * hidden_cols] = stacked[d, :, :hidden_cols]
                output_full[:, d * output_cols:(d + 1) * output_cols] = stacked[d, :, hidden_cols:]

        dims = (((1,), (1,)), ((), ()))
        left = lax.dot_general(hidden_ref[...], hidden_full[...], dims, preferred_element_type=jnp.float32)
        right = lax.dot_general(grad_ref[...], output_full[...], dims, preferred_element_type=jnp.float32)
        at = pl.multiple_of(step * tile, tile)
        rows[pl.ds(at, tile), :rank_width] = left.astype(jnp.bfloat16)
        rows[pl.ds(at, tile), rank_width:] = right.astype(jnp.bfloat16)

        @pl.when(step == pl.num_programs(0) - 1)
        def _():
            tokens, lanes = rows.shape
            rows_of = lambda ref: jnp.broadcast_to(ref[...].reshape(1, tokens).astype(jnp.float32), (8, tokens))
            columns = jnp.concatenate([rows_of(owner_ref), rows_of(slot_ref)], axis=0).T
            targets = columns[:, 0:1].astype(jnp.int32)
            slots = columns[:, 8:9]
            member = (targets == lax.broadcasted_iota(jnp.int32, (tokens, devices), 1)).astype(jnp.bfloat16)
            earlier = (
                lax.broadcasted_iota(jnp.int32, (tokens, tokens), 0)
                > lax.broadcasted_iota(jnp.int32, (tokens, tokens), 1)
            ).astype(jnp.bfloat16)
            before = jnp.dot(earlier, member, preferred_element_type=jnp.float32)
            position = jnp.sum(member.astype(jnp.float32) * before, axis=1, keepdims=True).astype(jnp.int32)
            slot_index = targets * capacity + position
            spread = (
                slot_index == lax.broadcasted_iota(jnp.int32, (tokens, devices * capacity), 1)
            ).astype(jnp.bfloat16)
            down = (((0,), (0,)), ((), ()))
            placed = lax.dot_general(spread, rows[...], down, preferred_element_type=jnp.float32)
            placed = placed.astype(jnp.bfloat16)
            tagged = member * (slots + 1.0).astype(jnp.bfloat16)
            spot = (position == lax.broadcasted_iota(jnp.int32, (tokens, lanes), 1)).astype(jnp.bfloat16)
            labels = lax.dot_general(tagged, spot, down, preferred_element_type=jnp.float32)
            labels = labels.astype(jnp.bfloat16)
            for d in range(devices):
                out_ref[d, :capacity, :] = placed[d * capacity:(d + 1) * capacity, :]
                out_ref[d, capacity:, :] = labels[d:d + 1, :]

    return kernel


def project_rows(blocks, other, table, hidden, out_grad, owner_ids, doc_slot, devices, capacity):
    count = len(blocks)
    paired = other is not None
    rank_width, width = blocks[0].shape
    local_tokens, features = hidden.shape
    outputs = out_grad.shape[1]
    tile = 128 if local_tokens % 128 == 0 else local_tokens
    whole = pl.BlockSpec((rank_width, width), lambda i, table: (0, 0))
    grid_spec = pltpu.PrefetchScalarGridSpec(
        num_scalar_prefetch=1,
        grid=(local_tokens // tile,),
        in_specs=[whole] * count + [pl.BlockSpec((count, rank_width, width), lambda i, table: (0, 0, 0))] * paired + [
            pl.BlockSpec((tile, features), lambda i, table: (i, 0)),
            pl.BlockSpec((tile, outputs), lambda i, table: (i, 0)),
            pl.BlockSpec((1, local_tokens), lambda i, table: (0, 0)),
            pl.BlockSpec((local_tokens,), lambda i, table: (0,)),
        ],
        out_specs=pl.BlockSpec((devices, capacity + 1, 2 * rank_width), lambda i, table: (0, 0, 0)),
        scratch_shapes=[
            pltpu.VMEM((local_tokens, 2 * rank_width), jnp.bfloat16),
            pltpu.VMEM((devices, rank_width, width), jnp.bfloat16),
            pltpu.VMEM((rank_width, features), jnp.bfloat16),
            pltpu.VMEM((rank_width, outputs), jnp.bfloat16),
        ],
    )
    return pl.pallas_call(
        projection_kernel(count, devices, features // devices, outputs // devices, rank_width, paired, capacity),
        grid_spec=grid_spec,
        out_shape=jax.ShapeDtypeStruct((devices, capacity + 1, 2 * rank_width), jnp.bfloat16),
        compiler_params=pltpu.CompilerParams(dimension_semantics=("arbitrary",)),
    )(table, *blocks, *([other] if paired else []), hidden, out_grad, owner_ids.reshape(1, -1), doc_slot)


def local(hidden, out_grad, hidden_basis, output_basis, owner_ids, doc_slot):
    devices = lax.axis_size("dp")
    local_tokens = hidden.shape[0]
    capacity = 2 * local_tokens // devices
    rank_width = hidden_basis.shape[0]
    buffer_len = devices * capacity
    blocks, other, table = ring_gather(jnp.concatenate([hidden_basis, output_basis], axis=1), devices)
    packed = project_rows(blocks, other, table, hidden, out_grad, owner_ids, doc_slot, devices, capacity)
    arrived = lax.all_to_all(packed, "dp", 0, 0, tiled=True)
    rows_in = arrived[:, :capacity, :].reshape(buffer_len, 2 * rank_width)
    label_in = arrived[:, capacity, :capacity].reshape(buffer_len, 1)
    left_in = rows_in[:, :rank_width]
    right_in = rows_in[:, rank_width:]
    wanted = (jnp.arange(DOCS_DEV, dtype=jnp.int32) + 1).astype(jnp.bfloat16)[None, :]
    selector = (label_in == wanted).astype(jnp.bfloat16)
    weighted = (selector[:, :, None] * left_in[:, None, :]).reshape(buffer_len, DOCS_DEV * rank_width)
    grads = lax.dot_general(
        weighted, right_in, (((0,), (0,)), ((), ())), preferred_element_type=jnp.float32
    )
    return grads.reshape(DOCS_DEV, rank_width * rank_width)


def solution(mesh):
    placed = (
        P(("groups", "dp"), None),
        P(("groups", "dp"), None),
        P(None, "dp"),
        P(None, "dp"),
        P(("groups", "dp"), None),
        P(("groups", "dp")),
    )
    return jax.shard_map(
        local, mesh=mesh, in_specs=placed, out_specs=P(("groups", "dp"), None), check_vma=False
    )
```

```python
import numpy as np
import jax
import jax.numpy as jnp
from jax import lax
from jax.experimental import pallas as pl
from jax.experimental.pallas import tpu as pltpu
from jax.sharding import PartitionSpec as P

DOCS_DEV = 8


def ring_planes(devices):
    chips = devices // 2
    if devices % 2 or chips < 2:
        return [list(range(devices))]
    if chips % 2 == 0 and chips >= 4:
        order = list(range(0, chips, 2)) + list(range(chips - 1, 0, -2))
    else:
        order = list(range(chips))
    return [[2 * chip + core for chip in order] for core in range(2)]


def ring_gather(block, devices):
    planes = ring_planes(devices)
    length = len(planes[0])
    place = np.zeros(devices, np.int32)
    plane_of = np.zeros(devices, np.int32)
    for plane, members in enumerate(planes):
        for spot, member in enumerate(members):
            place[member] = spot
            plane_of[member] = plane
    forward = [(ring[t], ring[(t + 1) % length]) for ring in planes for t in range(length)]
    backward = [(ring[t], ring[(t - 1) % length]) for ring in planes for t in range(length)]
    blocks = [block]
    shifts = [0]
    moving = block
    for step in range(1, length // 2 + 1):
        moving = lax.ppermute(moving, "dp", forward)
        blocks.append(moving)
        shifts.append(-step)
    moving = block
    for step in range(1, length - length // 2):
        moving = lax.ppermute(moving, "dp", backward)
        blocks.append(moving)
        shifts.append(step)
    table = np.zeros((devices, len(shifts) * len(planes)), np.int32)
    for member in range(devices):
        for k, shift in enumerate(shifts):
            for side in range(len(planes)):
                ring = planes[(plane_of[member] + side) % len(planes)]
                table[member, side * len(shifts) + k] = ring[(place[member] + shift) % length]
    owners = jnp.asarray(table.reshape(-1))
    if len(planes) == 1:
        return blocks, None, owners
    mine = jnp.stack(blocks)
    swap = list(zip(planes[0], planes[1])) + list(zip(planes[1], planes[0]))
    other = lax.ppermute(mine, "dp", swap)
    return blocks, other, owners


def projection_kernel(count, devices, hidden_cols, output_cols, rank_width, paired, capacity):
    width = count * (2 if paired else 1)

    def kernel(table, *refs):
        blocks = refs[:count]
        rest = refs[count:]
        if paired:
            other_ref, rest = rest[0], rest[1:]
        hidden_ref, grad_ref, owner_ref, slot_ref, out_ref, rows, stacked, hidden_full, output_full = rest
        step = pl.program_id(0)
        tile = hidden_ref.shape[0]
        me = lax.axis_index("dp")

        @pl.when(step == 0)
        def _():
            for k in range(count):
                stacked[table[me * width + k]] = blocks[k][...]
                if paired:
                    stacked[table[me * width + count + k]] = other_ref[k]
            for d in range(devices):
                hidden_full[:, d * hidden_cols:(d + 1) * hidden_cols] = stacked[d, :, :hidden_cols]
                output_full[:, d * output_cols:(d + 1) * output_cols] = stacked[d, :, hidden_cols:]

        dims = (((1,), (1,)), ((), ()))
        left = lax.dot_general(hidden_ref[...], hidden_full[...], dims, preferred_element_type=jnp.float32)
        right = lax.dot_general(grad_ref[...], output_full[...], dims, preferred_element_type=jnp.float32)
        at = pl.multiple_of(step * tile, tile)
        rows[pl.ds(at, tile), :rank_width] = left.astype(jnp.bfloat16)
        rows[pl.ds(at, tile), rank_width:] = right.astype(jnp.bfloat16)

        @pl.when(step == pl.num_programs(0) - 1)
        def _():
            tokens, lanes = rows.shape
            rows_of = lambda ref: jnp.broadcast_to(ref[...].reshape(1, tokens).astype(jnp.float32), (8, tokens))
            columns = jnp.concatenate([rows_of(owner_ref), rows_of(slot_ref)], axis=0).T
            targets = columns[:, 0:1].astype(jnp.int32)
            slots = columns[:, 8:9]
            member = (targets == lax.broadcasted_iota(jnp.int32, (tokens, devices), 1)).astype(jnp.bfloat16)
            earlier = (
                lax.broadcasted_iota(jnp.int32, (tokens, tokens), 0)
                > lax.broadcasted_iota(jnp.int32, (tokens, tokens), 1)
            ).astype(jnp.bfloat16)
            before = jnp.dot(earlier, member, preferred_element_type=jnp.float32)
            position = jnp.sum(member.astype(jnp.float32) * before, axis=1, keepdims=True).astype(jnp.int32)
            slot_index = targets * capacity + position
            spread = (
                slot_index == lax.broadcasted_iota(jnp.int32, (tokens, devices * capacity), 1)
            ).astype(jnp.bfloat16)
            down = (((0,), (0,)), ((), ()))
            placed = lax.dot_general(spread, rows[...], down, preferred_element_type=jnp.float32)
            placed = placed.astype(jnp.bfloat16)
            tagged = member * (slots + 1.0).astype(jnp.bfloat16)
            spot = (position == lax.broadcasted_iota(jnp.int32, (tokens, lanes), 1)).astype(jnp.bfloat16)
            labels = lax.dot_general(tagged, spot, down, preferred_element_type=jnp.float32)
            labels = labels.astype(jnp.bfloat16)
            for d in range(devices):
                out_ref[d, :capacity, :] = placed[d * capacity:(d + 1) * capacity, :]
                out_ref[d, capacity:, :] = labels[d:d + 1, :]

    return kernel


def project_rows(blocks, other, table, hidden, out_grad, owner_ids, doc_slot, devices, capacity):
    count = len(blocks)
    paired = other is not None
    rank_width, width = blocks[0].shape
    local_tokens, features = hidden.shape
    outputs = out_grad.shape[1]
    tile = 128 if local_tokens % 128 == 0 else local_tokens
    whole = pl.BlockSpec((rank_width, width), lambda i, table: (0, 0))
    grid_spec = pltpu.PrefetchScalarGridSpec(
        num_scalar_prefetch=1,
        grid=(local_tokens // tile,),
        in_specs=[whole] * count + [pl.BlockSpec((count, rank_width, width), lambda i, table: (0, 0, 0))] * paired + [
            pl.BlockSpec((tile, features), lambda i, table: (i, 0)),
            pl.BlockSpec((tile, outputs), lambda i, table: (i, 0)),
            pl.BlockSpec((1, local_tokens), lambda i, table: (0, 0)),
            pl.BlockSpec((local_tokens,), lambda i, table: (0,)),
        ],
        out_specs=pl.BlockSpec((devices, capacity + 1, 2 * rank_width), lambda i, table: (0, 0, 0)),
        scratch_shapes=[
            pltpu.VMEM((local_tokens, 2 * rank_width), jnp.bfloat16),
            pltpu.VMEM((devices, rank_width, width), jnp.bfloat16),
            pltpu.VMEM((rank_width, features), jnp.bfloat16),
            pltpu.VMEM((rank_width, outputs), jnp.bfloat16),
        ],
    )
    return pl.pallas_call(
        projection_kernel(count, devices, features // devices, outputs // devices, rank_width, paired, capacity),
        grid_spec=grid_spec,
        out_shape=jax.ShapeDtypeStruct((devices, capacity + 1, 2 * rank_width), jnp.bfloat16),
        compiler_params=pltpu.CompilerParams(dimension_semantics=("arbitrary",)),
    )(table, *blocks, *([other] if paired else []), hidden, out_grad, owner_ids.reshape(1, -1), doc_slot)


def half_kernel(count, hidden_cols, output_cols, rank_width, first, capacity, devices):
    def kernel(table, *refs):
        if first:
            blocks = refs[:count]
            hidden_ref, grad_ref, acc_ref, stacked = refs[count:]
        else:
            other_ref, hidden_ref, grad_ref, part_ref, owner_ref, slot_ref, out_ref, rows, stacked = refs
        step = pl.program_id(0)
        tile = hidden_ref.shape[0]
        me = lax.axis_index("dp")
        core = me % 2

        @pl.when(step == 0)
        def _():
            for k in range(count):
                if first:
                    stacked[table[me * 2 * count + k] // 2] = blocks[k][...]
                else:
                    stacked[table[me * 2 * count + count + k] // 2] = other_ref[k]

        dims = (((1,), (1,)), ((), ()))

        def partial(side):
            left = None
            right = None
            for chip in range(count):
                d = 2 * chip + side
                part = stacked[chip]
                one = lax.dot_general(
                    hidden_ref[:, d * hidden_cols:(d + 1) * hidden_cols], part[:, :hidden_cols], dims,
                    preferred_element_type=jnp.float32,
                )
                two = lax.dot_general(
                    grad_ref[:, d * output_cols:(d + 1) * output_cols], part[:, hidden_cols:], dims,
                    preferred_element_type=jnp.float32,
                )
                left = one if left is None else left + one
                right = two if right is None else right + two
            return jnp.concatenate([left, right], axis=1)

        mine_side = core if first else 1 - core
        summed = lax.cond(mine_side == 0, lambda: partial(0), lambda: partial(1))
        if first:
            acc_ref[...] = summed
            return
        at = pl.multiple_of(step * tile, tile)
        rows[pl.ds(at, tile), :] = (summed + part_ref[...]).astype(jnp.bfloat16)

        @pl.when(step == pl.num_programs(0) - 1)
        def _():
            tokens, lanes = rows.shape
            rows_of = lambda ref: jnp.broadcast_to(ref[...].reshape(1, tokens).astype(jnp.float32), (8, tokens))
            columns = jnp.concatenate([rows_of(owner_ref), rows_of(slot_ref)], axis=0).T
            targets = columns[:, 0:1].astype(jnp.int32)
            slots = columns[:, 8:9]
            member = (targets == lax.broadcasted_iota(jnp.int32, (tokens, devices), 1)).astype(jnp.bfloat16)
            earlier = (
                lax.broadcasted_iota(jnp.int32, (tokens, tokens), 0)
                > lax.broadcasted_iota(jnp.int32, (tokens, tokens), 1)
            ).astype(jnp.bfloat16)
            before = jnp.dot(earlier, member, preferred_element_type=jnp.float32)
            position = jnp.sum(member.astype(jnp.float32) * before, axis=1, keepdims=True).astype(jnp.int32)
            slot_index = targets * capacity + position
            spread = (
                slot_index == lax.broadcasted_iota(jnp.int32, (tokens, devices * capacity), 1)
            ).astype(jnp.bfloat16)
            down = (((0,), (0,)), ((), ()))
            placed = lax.dot_general(spread, rows[...], down, preferred_element_type=jnp.float32)
            placed = placed.astype(jnp.bfloat16)
            tagged = member * (slots + 1.0).astype(jnp.bfloat16)
            spot = (position == lax.broadcasted_iota(jnp.int32, (tokens, lanes), 1)).astype(jnp.bfloat16)
            labels = lax.dot_general(tagged, spot, down, preferred_element_type=jnp.float32)
            labels = labels.astype(jnp.bfloat16)
            for d in range(devices):
                out_ref[d, :capacity, :] = placed[d * capacity:(d + 1) * capacity, :]
                out_ref[d, capacity:, :] = labels[d:d + 1, :]

    return kernel


def project_in_halves(blocks, other, table, hidden, out_grad, owner_ids, doc_slot, devices, capacity):
    count = len(blocks)
    rank_width, width = blocks[0].shape
    local_tokens, features = hidden.shape
    outputs = out_grad.shape[1]
    tile = 128 if local_tokens % 128 == 0 else local_tokens
    grid = (local_tokens // tile,)
    token_specs = [
        pl.BlockSpec((tile, features), lambda i, table: (i, 0)),
        pl.BlockSpec((tile, outputs), lambda i, table: (i, 0)),
    ]
    part_spec = pl.BlockSpec((tile, 2 * rank_width), lambda i, table: (i, 0))
    stacked = pltpu.VMEM((count, rank_width, width), jnp.bfloat16)
    params = pltpu.CompilerParams(dimension_semantics=("arbitrary",))
    shape = (features // devices, outputs // devices, rank_width)
    first = pl.pallas_call(
        half_kernel(count, *shape, True, capacity, devices),
        grid_spec=pltpu.PrefetchScalarGridSpec(
            num_scalar_prefetch=1,
            grid=grid,
            in_specs=[pl.BlockSpec((rank_width, width), lambda i, table: (0, 0))] * count + token_specs,
            out_specs=part_spec,
            scratch_shapes=[stacked],
        ),
        out_shape=jax.ShapeDtypeStruct((local_tokens, 2 * rank_width), jnp.float32),
        compiler_params=params,
    )(table, *blocks, hidden, out_grad)
    return pl.pallas_call(
        half_kernel(count, *shape, False, capacity, devices),
        grid_spec=pltpu.PrefetchScalarGridSpec(
            num_scalar_prefetch=1,
            grid=grid,
            in_specs=[pl.BlockSpec((count, rank_width, width), lambda i, table: (0, 0, 0))] + token_specs + [
                part_spec,
                pl.BlockSpec((1, local_tokens), lambda i, table: (0, 0)),
                pl.BlockSpec((local_tokens,), lambda i, table: (0,)),
            ],
            out_specs=pl.BlockSpec((devices, capacity + 1, 2 * rank_width), lambda i, table: (0, 0, 0)),
            scratch_shapes=[pltpu.VMEM((local_tokens, 2 * rank_width), jnp.bfloat16), stacked],
        ),
        out_shape=jax.ShapeDtypeStruct((devices, capacity + 1, 2 * rank_width), jnp.bfloat16),
        compiler_params=params,
    )(table, other, hidden, out_grad, first, owner_ids.reshape(1, -1), doc_slot)


def local(hidden, out_grad, hidden_basis, output_basis, owner_ids, doc_slot):
    devices = lax.axis_size("dp")
    local_tokens = hidden.shape[0]
    capacity = 2 * local_tokens // devices
    rank_width = hidden_basis.shape[0]
    buffer_len = devices * capacity
    blocks, other, table = ring_gather(jnp.concatenate([hidden_basis, output_basis], axis=1), devices)
    if other is None:
        packed = project_rows(blocks, other, table, hidden, out_grad, owner_ids, doc_slot, devices, capacity)
    else:
        packed = project_in_halves(blocks, other, table, hidden, out_grad, owner_ids, doc_slot, devices, capacity)
    arrived = lax.all_to_all(packed, "dp", 0, 0, tiled=True)
    rows_in = arrived[:, :capacity, :].reshape(buffer_len, 2 * rank_width)
    label_in = arrived[:, capacity, :capacity].reshape(buffer_len, 1)
    left_in = rows_in[:, :rank_width]
    right_in = rows_in[:, rank_width:]
    wanted = (jnp.arange(DOCS_DEV, dtype=jnp.int32) + 1).astype(jnp.bfloat16)[None, :]
    selector = (label_in == wanted).astype(jnp.bfloat16)
    weighted = (selector[:, :, None] * left_in[:, None, :]).reshape(buffer_len, DOCS_DEV * rank_width)
    grads = lax.dot_general(
        weighted, right_in, (((0,), (0,)), ((), ())), preferred_element_type=jnp.float32
    )
    return grads.reshape(DOCS_DEV, rank_width * rank_width)


def solution(mesh):
    placed = (
        P(("groups", "dp"), None),
        P(("groups", "dp"), None),
        P(None, "dp"),
        P(None, "dp"),
        P(("groups", "dp"), None),
        P(("groups", "dp")),
    )
    return jax.shard_map(
        local, mesh=mesh, in_specs=placed, out_specs=P(("groups", "dp"), None), check_vma=False
    )
```

```python
import numpy as np
import jax
import jax.numpy as jnp
from jax import lax
from jax.experimental import pallas as pl
from jax.experimental.pallas import tpu as pltpu
from jax.sharding import PartitionSpec as P

DOCS_DEV = 8


def ring_planes(devices):
    chips = devices // 2
    if devices % 2 or chips < 2:
        return [list(range(devices))]
    if chips % 2 == 0 and chips >= 4:
        order = list(range(0, chips, 2)) + list(range(chips - 1, 0, -2))
    else:
        order = list(range(chips))
    return [[2 * chip + core for chip in order] for core in range(2)]


def ring_gather(block, devices):
    planes = ring_planes(devices)
    length = len(planes[0])
    place = np.zeros(devices, np.int32)
    plane_of = np.zeros(devices, np.int32)
    for plane, members in enumerate(planes):
        for spot, member in enumerate(members):
            place[member] = spot
            plane_of[member] = plane
    forward = [(ring[t], ring[(t + 1) % length]) for ring in planes for t in range(length)]
    backward = [(ring[t], ring[(t - 1) % length]) for ring in planes for t in range(length)]
    blocks = [block]
    shifts = [0]
    moving = block
    for step in range(1, length // 2 + 1):
        moving = lax.ppermute(moving, "dp", forward)
        blocks.append(moving)
        shifts.append(-step)
    moving = block
    for step in range(1, length - length // 2):
        moving = lax.ppermute(moving, "dp", backward)
        blocks.append(moving)
        shifts.append(step)
    table = np.zeros((devices, len(shifts) * len(planes)), np.int32)
    for member in range(devices):
        for k, shift in enumerate(shifts):
            for side in range(len(planes)):
                ring = planes[(plane_of[member] + side) % len(planes)]
                table[member, side * len(shifts) + k] = ring[(place[member] + shift) % length]
    owners = jnp.asarray(table.reshape(-1))
    if len(planes) == 1:
        return blocks, None, owners
    mine = jnp.stack(blocks)
    swap = list(zip(planes[0], planes[1])) + list(zip(planes[1], planes[0]))
    other = lax.ppermute(mine, "dp", swap)
    return blocks, other, owners


def projection_kernel(count, devices, hidden_cols, output_cols, rank_width, paired, capacity):
    width = count * (2 if paired else 1)

    def kernel(table, *refs):
        blocks = refs[:count]
        rest = refs[count:]
        if paired:
            other_ref, rest = rest[0], rest[1:]
        hidden_ref, grad_ref, owner_ref, slot_ref, out_ref, rows, stacked, hidden_full, output_full = rest
        step = pl.program_id(0)
        tile = hidden_ref.shape[0]
        me = lax.axis_index("dp")

        @pl.when(step == 0)
        def _():
            for k in range(count):
                stacked[table[me * width + k]] = blocks[k][...]
                if paired:
                    stacked[table[me * width + count + k]] = other_ref[k]
            for d in range(devices):
                hidden_full[:, d * hidden_cols:(d + 1) * hidden_cols] = stacked[d, :, :hidden_cols]
                output_full[:, d * output_cols:(d + 1) * output_cols] = stacked[d, :, hidden_cols:]

        dims = (((1,), (1,)), ((), ()))
        left = lax.dot_general(hidden_full[...], hidden_ref[...], dims, preferred_element_type=jnp.float32)
        right = lax.dot_general(output_full[...], grad_ref[...], dims, preferred_element_type=jnp.float32)
        at = pl.multiple_of(step * tile, tile)
        rows[:rank_width, pl.ds(at, tile)] = left.astype(jnp.bfloat16)
        rows[rank_width:, pl.ds(at, tile)] = right.astype(jnp.bfloat16)

        @pl.when(step == pl.num_programs(0) - 1)
        def _():
            lanes, tokens = rows.shape
            targets = owner_ref[...]
            slots = slot_ref[...].reshape(1, tokens)
            member = (targets == lax.broadcasted_iota(jnp.int32, (devices, tokens), 0)).astype(jnp.bfloat16)
            later = (
                lax.broadcasted_iota(jnp.int32, (tokens, tokens), 0)
                < lax.broadcasted_iota(jnp.int32, (tokens, tokens), 1)
            ).astype(jnp.bfloat16)
            before = jnp.dot(member, later, preferred_element_type=jnp.float32)
            position = jnp.sum(member.astype(jnp.float32) * before, axis=0, keepdims=True).astype(jnp.int32)
            slot_index = targets * capacity + position
            spread = (
                lax.broadcasted_iota(jnp.int32, (devices * capacity, tokens), 0) == slot_index
            ).astype(jnp.bfloat16)
            placed = lax.dot_general(spread, rows[...], dims, preferred_element_type=jnp.float32)
            placed = placed.astype(jnp.bfloat16)
            tagged = member * (slots + 1).astype(jnp.bfloat16)
            spot = (lax.broadcasted_iota(jnp.int32, (lanes, tokens), 0) == position).astype(jnp.bfloat16)
            labels = lax.dot_general(tagged, spot, dims, preferred_element_type=jnp.float32)
            labels = labels.astype(jnp.bfloat16)
            for d in range(devices):
                out_ref[d, :capacity, :] = placed[d * capacity:(d + 1) * capacity, :]
                out_ref[d, capacity:, :] = labels[d:d + 1, :]

    return kernel


def project_rows(blocks, other, table, hidden, out_grad, owner_ids, doc_slot, devices, capacity):
    count = len(blocks)
    paired = other is not None
    rank_width, width = blocks[0].shape
    local_tokens, features = hidden.shape
    outputs = out_grad.shape[1]
    tile = 128 if local_tokens % 128 == 0 else local_tokens
    whole = pl.BlockSpec((rank_width, width), lambda i, table: (0, 0))
    grid_spec = pltpu.PrefetchScalarGridSpec(
        num_scalar_prefetch=1,
        grid=(local_tokens // tile,),
        in_specs=[whole] * count + [pl.BlockSpec((count, rank_width, width), lambda i, table: (0, 0, 0))] * paired + [
            pl.BlockSpec((tile, features), lambda i, table: (i, 0)),
            pl.BlockSpec((tile, outputs), lambda i, table: (i, 0)),
            pl.BlockSpec((1, local_tokens), lambda i, table: (0, 0)),
            pl.BlockSpec((local_tokens,), lambda i, table: (0,)),
        ],
        out_specs=pl.BlockSpec((devices, capacity + 1, 2 * rank_width), lambda i, table: (0, 0, 0)),
        scratch_shapes=[
            pltpu.VMEM((2 * rank_width, local_tokens), jnp.bfloat16),
            pltpu.VMEM((devices, rank_width, width), jnp.bfloat16),
            pltpu.VMEM((rank_width, features), jnp.bfloat16),
            pltpu.VMEM((rank_width, outputs), jnp.bfloat16),
        ],
    )
    return pl.pallas_call(
        projection_kernel(count, devices, features // devices, outputs // devices, rank_width, paired, capacity),
        grid_spec=grid_spec,
        out_shape=jax.ShapeDtypeStruct((devices, capacity + 1, 2 * rank_width), jnp.bfloat16),
        compiler_params=pltpu.CompilerParams(dimension_semantics=("arbitrary",)),
    )(table, *blocks, *([other] if paired else []), hidden, out_grad, owner_ids.reshape(1, -1), doc_slot)


def local(hidden, out_grad, hidden_basis, output_basis, owner_ids, doc_slot):
    devices = lax.axis_size("dp")
    local_tokens = hidden.shape[0]
    capacity = 2 * local_tokens // devices
    rank_width = hidden_basis.shape[0]
    buffer_len = devices * capacity
    blocks, other, table = ring_gather(jnp.concatenate([hidden_basis, output_basis], axis=1), devices)
    packed = project_rows(blocks, other, table, hidden, out_grad, owner_ids, doc_slot, devices, capacity)
    arrived = lax.all_to_all(packed, "dp", 0, 0, tiled=True)
    rows_in = arrived[:, :capacity, :].reshape(buffer_len, 2 * rank_width)
    label_in = arrived[:, capacity, :capacity].reshape(buffer_len, 1)
    left_in = rows_in[:, :rank_width]
    right_in = rows_in[:, rank_width:]
    wanted = (jnp.arange(DOCS_DEV, dtype=jnp.int32) + 1).astype(jnp.bfloat16)[None, :]
    selector = (label_in == wanted).astype(jnp.bfloat16)
    weighted = (selector[:, :, None] * left_in[:, None, :]).reshape(buffer_len, DOCS_DEV * rank_width)
    grads = lax.dot_general(
        weighted, right_in, (((0,), (0,)), ((), ())), preferred_element_type=jnp.float32
    )
    return grads.reshape(DOCS_DEV, rank_width * rank_width)


def solution(mesh):
    placed = (
        P(("groups", "dp"), None),
        P(("groups", "dp"), None),
        P(None, "dp"),
        P(None, "dp"),
        P(("groups", "dp"), None),
        P(("groups", "dp")),
    )
    return jax.shard_map(
        local, mesh=mesh, in_specs=placed, out_specs=P(("groups", "dp"), None), check_vma=False
    )
```

```python
import numpy as np
import jax
import jax.numpy as jnp
from jax import lax
from jax.experimental import pallas as pl
from jax.experimental.pallas import tpu as pltpu
from jax.sharding import PartitionSpec as P

DOCS_DEV = 8


def ring_planes(devices):
    chips = devices // 2
    if devices % 2 or chips < 2:
        return [list(range(devices))]
    if chips % 2 == 0 and chips >= 4:
        order = list(range(0, chips, 2)) + list(range(chips - 1, 0, -2))
    else:
        order = list(range(chips))
    return [[2 * chip + core for chip in order] for core in range(2)]


def ring_gather(block, devices):
    planes = ring_planes(devices)
    length = len(planes[0])
    place = np.zeros(devices, np.int32)
    plane_of = np.zeros(devices, np.int32)
    for plane, members in enumerate(planes):
        for spot, member in enumerate(members):
            place[member] = spot
            plane_of[member] = plane
    forward = [(ring[t], ring[(t + 1) % length]) for ring in planes for t in range(length)]
    backward = [(ring[t], ring[(t - 1) % length]) for ring in planes for t in range(length)]
    early, late = [block], []
    early_shifts, late_shifts = [0], []
    split = max(1, length // 4)
    ahead = behind = block
    for step in range(1, length // 2 + 1):
        ahead = lax.ppermute(ahead, "dp", forward)
        (early if step <= split else late).append(ahead)
        (early_shifts if step <= split else late_shifts).append(-step)
        if step < length - length // 2:
            behind = lax.ppermute(behind, "dp", backward)
            (early if step <= split else late).append(behind)
            (early_shifts if step <= split else late_shifts).append(step)
    blocks = early + late
    shifts = early_shifts + late_shifts
    table = np.zeros((devices, len(shifts) * len(planes)), np.int32)
    for member in range(devices):
        for k, shift in enumerate(shifts):
            for side in range(len(planes)):
                ring = planes[(plane_of[member] + side) % len(planes)]
                table[member, side * len(shifts) + k] = ring[(place[member] + shift) % length]
    owners = jnp.asarray(table.reshape(-1))
    if len(planes) == 1:
        return blocks, None, owners
    swap = list(zip(planes[0], planes[1])) + list(zip(planes[1], planes[0]))
    other = [lax.ppermute(jnp.stack(group), "dp", swap) for group in (early, late) if group]
    return blocks, other, owners


def projection_kernel(count, devices, hidden_cols, output_cols, rank_width, paired, capacity):
    width = count * (2 if paired else 1)

    def kernel(table, *refs):
        blocks = refs[:count]
        rest = refs[count:]
        if paired:
            other_refs, rest = rest[:len(paired)], rest[len(paired):]
        hidden_ref, grad_ref, owner_ref, slot_ref, out_ref, rows, stacked, hidden_full, output_full = rest
        step = pl.program_id(0)
        tile = hidden_ref.shape[0]
        me = lax.axis_index("dp")

        @pl.when(step == 0)
        def _():
            for k in range(count):
                stacked[table[me * width + k]] = blocks[k][...]
            at = count
            for other_ref, size in zip(other_refs if paired else (), paired):
                for k in range(size):
                    stacked[table[me * width + at + k]] = other_ref[k]
                at += size
            for d in range(devices):
                hidden_full[:, d * hidden_cols:(d + 1) * hidden_cols] = stacked[d, :, :hidden_cols]
                output_full[:, d * output_cols:(d + 1) * output_cols] = stacked[d, :, hidden_cols:]

        dims = (((1,), (1,)), ((), ()))
        left = lax.dot_general(hidden_full[...], hidden_ref[...], dims, preferred_element_type=jnp.float32)
        right = lax.dot_general(output_full[...], grad_ref[...], dims, preferred_element_type=jnp.float32)
        at = pl.multiple_of(step * tile, tile)
        rows[:rank_width, pl.ds(at, tile)] = left.astype(jnp.bfloat16)
        rows[rank_width:, pl.ds(at, tile)] = right.astype(jnp.bfloat16)

        @pl.when(step == pl.num_programs(0) - 1)
        def _():
            lanes, tokens = rows.shape
            targets = owner_ref[...]
            slots = slot_ref[...].reshape(1, tokens)
            member = (targets == lax.broadcasted_iota(jnp.int32, (devices, tokens), 0)).astype(jnp.bfloat16)
            later = (
                lax.broadcasted_iota(jnp.int32, (tokens, tokens), 0)
                < lax.broadcasted_iota(jnp.int32, (tokens, tokens), 1)
            ).astype(jnp.bfloat16)
            before = jnp.dot(member, later, preferred_element_type=jnp.float32)
            position = jnp.sum(member.astype(jnp.float32) * before, axis=0, keepdims=True).astype(jnp.int32)
            slot_index = targets * capacity + position
            spread = (
                lax.broadcasted_iota(jnp.int32, (devices * capacity, tokens), 0) == slot_index
            ).astype(jnp.bfloat16)
            placed = lax.dot_general(spread, rows[...], dims, preferred_element_type=jnp.float32)
            placed = placed.astype(jnp.bfloat16)
            tagged = member * (slots + 1).astype(jnp.bfloat16)
            spot = (lax.broadcasted_iota(jnp.int32, (lanes, tokens), 0) == position).astype(jnp.bfloat16)
            labels = lax.dot_general(tagged, spot, dims, preferred_element_type=jnp.float32)
            labels = labels.astype(jnp.bfloat16)
            for d in range(devices):
                out_ref[d, :capacity, :] = placed[d * capacity:(d + 1) * capacity, :]
                out_ref[d, capacity:, :] = labels[d:d + 1, :]

    return kernel


def project_rows(blocks, other, table, hidden, out_grad, owner_ids, doc_slot, devices, capacity):
    count = len(blocks)
    paired = tuple(part.shape[0] for part in other) if other is not None else ()
    rank_width, width = blocks[0].shape
    local_tokens, features = hidden.shape
    outputs = out_grad.shape[1]
    tile = 128 if local_tokens % 128 == 0 else local_tokens
    whole = pl.BlockSpec((rank_width, width), lambda i, table: (0, 0))
    grid_spec = pltpu.PrefetchScalarGridSpec(
        num_scalar_prefetch=1,
        grid=(local_tokens // tile,),
        in_specs=[whole] * count + [pl.BlockSpec(part.shape, lambda i, table: (0, 0, 0)) for part in (other or [])] + [
            pl.BlockSpec((tile, features), lambda i, table: (i, 0)),
            pl.BlockSpec((tile, outputs), lambda i, table: (i, 0)),
            pl.BlockSpec((1, local_tokens), lambda i, table: (0, 0)),
            pl.BlockSpec((local_tokens,), lambda i, table: (0,)),
        ],
        out_specs=pl.BlockSpec((devices, capacity + 1, 2 * rank_width), lambda i, table: (0, 0, 0)),
        scratch_shapes=[
            pltpu.VMEM((2 * rank_width, local_tokens), jnp.bfloat16),
            pltpu.VMEM((devices, rank_width, width), jnp.bfloat16),
            pltpu.VMEM((rank_width, features), jnp.bfloat16),
            pltpu.VMEM((rank_width, outputs), jnp.bfloat16),
        ],
    )
    return pl.pallas_call(
        projection_kernel(count, devices, features // devices, outputs // devices, rank_width, paired, capacity),
        grid_spec=grid_spec,
        out_shape=jax.ShapeDtypeStruct((devices, capacity + 1, 2 * rank_width), jnp.bfloat16),
        compiler_params=pltpu.CompilerParams(dimension_semantics=("arbitrary",)),
    )(table, *blocks, *(other or []), hidden, out_grad, owner_ids.reshape(1, -1), doc_slot)


def local(hidden, out_grad, hidden_basis, output_basis, owner_ids, doc_slot):
    devices = lax.axis_size("dp")
    local_tokens = hidden.shape[0]
    capacity = 2 * local_tokens // devices
    rank_width = hidden_basis.shape[0]
    buffer_len = devices * capacity
    blocks, other, table = ring_gather(jnp.concatenate([hidden_basis, output_basis], axis=1), devices)
    packed = project_rows(blocks, other, table, hidden, out_grad, owner_ids, doc_slot, devices, capacity)
    arrived = lax.all_to_all(packed, "dp", 0, 0, tiled=True)
    rows_in = arrived[:, :capacity, :].reshape(buffer_len, 2 * rank_width)
    label_in = arrived[:, capacity, :capacity].reshape(buffer_len, 1)
    left_in = rows_in[:, :rank_width]
    right_in = rows_in[:, rank_width:]
    wanted = (jnp.arange(DOCS_DEV, dtype=jnp.int32) + 1).astype(jnp.bfloat16)[None, :]
    selector = (label_in == wanted).astype(jnp.bfloat16)
    weighted = (selector[:, :, None] * left_in[:, None, :]).reshape(buffer_len, DOCS_DEV * rank_width)
    grads = lax.dot_general(
        weighted, right_in, (((0,), (0,)), ((), ())), preferred_element_type=jnp.float32
    )
    return grads.reshape(DOCS_DEV, rank_width * rank_width)


def solution(mesh):
    placed = (
        P(("groups", "dp"), None),
        P(("groups", "dp"), None),
        P(None, "dp"),
        P(None, "dp"),
        P(("groups", "dp"), None),
        P(("groups", "dp")),
    )
    return jax.shard_map(
        local, mesh=mesh, in_specs=placed, out_specs=P(("groups", "dp"), None), check_vma=False
    )
```

```python
import numpy as np
import jax
import jax.numpy as jnp
from jax import lax
from jax.experimental import pallas as pl
from jax.experimental.pallas import tpu as pltpu
from jax.sharding import PartitionSpec as P

DOCS_DEV = 8


def ring_planes(devices):
    chips = devices // 2
    if devices % 2 or chips < 2:
        return [list(range(devices))]
    if chips % 2 == 0 and chips >= 4:
        order = list(range(0, chips, 2)) + list(range(chips - 1, 0, -2))
    else:
        order = list(range(chips))
    return [[2 * chip + core for chip in order] for core in range(2)]


def ring_gather(block, devices):
    planes = ring_planes(devices)
    length = len(planes[0])
    place = np.zeros(devices, np.int32)
    plane_of = np.zeros(devices, np.int32)
    for plane, members in enumerate(planes):
        for spot, member in enumerate(members):
            place[member] = spot
            plane_of[member] = plane
    forward = [(ring[t], ring[(t + 1) % length]) for ring in planes for t in range(length)]
    backward = [(ring[t], ring[(t - 1) % length]) for ring in planes for t in range(length)]
    early, late = [block], []
    early_shifts, late_shifts = [0], []
    split = max(1, length // 2 - 1)
    ahead = behind = block
    for step in range(1, length // 2 + 1):
        ahead = lax.ppermute(ahead, "dp", forward)
        (early if step <= split else late).append(ahead)
        (early_shifts if step <= split else late_shifts).append(-step)
        if step < length - length // 2:
            behind = lax.ppermute(behind, "dp", backward)
            (early if step <= split else late).append(behind)
            (early_shifts if step <= split else late_shifts).append(step)
    blocks = early + late
    shifts = early_shifts + late_shifts
    table = np.zeros((devices, len(shifts) * len(planes)), np.int32)
    for member in range(devices):
        for k, shift in enumerate(shifts):
            for side in range(len(planes)):
                ring = planes[(plane_of[member] + side) % len(planes)]
                table[member, side * len(shifts) + k] = ring[(place[member] + shift) % length]
    owners = jnp.asarray(table.reshape(-1))
    if len(planes) == 1:
        return blocks, None, owners
    swap = list(zip(planes[0], planes[1])) + list(zip(planes[1], planes[0]))
    other = [lax.ppermute(jnp.stack(group), "dp", swap) for group in (early, late) if group]
    return blocks, other, owners


def projection_kernel(count, devices, hidden_cols, output_cols, rank_width, paired, capacity):
    width = count * (2 if paired else 1)

    def kernel(table, *refs):
        blocks = refs[:count]
        rest = refs[count:]
        if paired:
            other_refs, rest = rest[:len(paired)], rest[len(paired):]
        hidden_ref, grad_ref, owner_ref, slot_ref, out_ref, rows, stacked, hidden_full, output_full = rest
        step = pl.program_id(0)
        tile = hidden_ref.shape[0]
        me = lax.axis_index("dp")

        @pl.when(step == 0)
        def _():
            for k in range(count):
                stacked[table[me * width + k]] = blocks[k][...]
            at = count
            for other_ref, size in zip(other_refs if paired else (), paired):
                for k in range(size):
                    stacked[table[me * width + at + k]] = other_ref[k]
                at += size
            for d in range(devices):
                hidden_full[:, d * hidden_cols:(d + 1) * hidden_cols] = stacked[d, :, :hidden_cols]
                output_full[:, d * output_cols:(d + 1) * output_cols] = stacked[d, :, hidden_cols:]

        dims = (((1,), (1,)), ((), ()))
        left = lax.dot_general(hidden_full[...], hidden_ref[...], dims, preferred_element_type=jnp.float32)
        right = lax.dot_general(output_full[...], grad_ref[...], dims, preferred_element_type=jnp.float32)
        at = pl.multiple_of(step * tile, tile)
        rows[:rank_width, pl.ds(at, tile)] = left.astype(jnp.bfloat16)
        rows[rank_width:, pl.ds(at, tile)] = right.astype(jnp.bfloat16)

        @pl.when(step == pl.num_programs(0) - 1)
        def _():
            lanes, tokens = rows.shape
            targets = owner_ref[...]
            slots = slot_ref[...].reshape(1, tokens)
            member = (targets == lax.broadcasted_iota(jnp.int32, (devices, tokens), 0)).astype(jnp.bfloat16)
            later = (
                lax.broadcasted_iota(jnp.int32, (tokens, tokens), 0)
                < lax.broadcasted_iota(jnp.int32, (tokens, tokens), 1)
            ).astype(jnp.bfloat16)
            before = jnp.dot(member, later, preferred_element_type=jnp.float32)
            position = jnp.sum(member.astype(jnp.float32) * before, axis=0, keepdims=True).astype(jnp.int32)
            slot_index = targets * capacity + position
            spread = (
                lax.broadcasted_iota(jnp.int32, (devices * capacity, tokens), 0) == slot_index
            ).astype(jnp.bfloat16)
            placed = lax.dot_general(spread, rows[...], dims, preferred_element_type=jnp.float32)
            placed = placed.astype(jnp.bfloat16)
            tagged = member * (slots + 1).astype(jnp.bfloat16)
            spot = (lax.broadcasted_iota(jnp.int32, (lanes, tokens), 0) == position).astype(jnp.bfloat16)
            labels = lax.dot_general(tagged, spot, dims, preferred_element_type=jnp.float32)
            labels = labels.astype(jnp.bfloat16)
            for d in range(devices):
                out_ref[d, :capacity, :] = placed[d * capacity:(d + 1) * capacity, :]
                out_ref[d, capacity:, :] = labels[d:d + 1, :]

    return kernel


def project_rows(blocks, other, table, hidden, out_grad, owner_ids, doc_slot, devices, capacity):
    count = len(blocks)
    paired = tuple(part.shape[0] for part in other) if other is not None else ()
    rank_width, width = blocks[0].shape
    local_tokens, features = hidden.shape
    outputs = out_grad.shape[1]
    tile = 128 if local_tokens % 128 == 0 else local_tokens
    whole = pl.BlockSpec((rank_width, width), lambda i, table: (0, 0))
    grid_spec = pltpu.PrefetchScalarGridSpec(
        num_scalar_prefetch=1,
        grid=(local_tokens // tile,),
        in_specs=[whole] * count + [pl.BlockSpec(part.shape, lambda i, table: (0, 0, 0)) for part in (other or [])] + [
            pl.BlockSpec((tile, features), lambda i, table: (i, 0)),
            pl.BlockSpec((tile, outputs), lambda i, table: (i, 0)),
            pl.BlockSpec((1, local_tokens), lambda i, table: (0, 0)),
            pl.BlockSpec((local_tokens,), lambda i, table: (0,)),
        ],
        out_specs=pl.BlockSpec((devices, capacity + 1, 2 * rank_width), lambda i, table: (0, 0, 0)),
        scratch_shapes=[
            pltpu.VMEM((2 * rank_width, local_tokens), jnp.bfloat16),
            pltpu.VMEM((devices, rank_width, width), jnp.bfloat16),
            pltpu.VMEM((rank_width, features), jnp.bfloat16),
            pltpu.VMEM((rank_width, outputs), jnp.bfloat16),
        ],
    )
    return pl.pallas_call(
        projection_kernel(count, devices, features // devices, outputs // devices, rank_width, paired, capacity),
        grid_spec=grid_spec,
        out_shape=jax.ShapeDtypeStruct((devices, capacity + 1, 2 * rank_width), jnp.bfloat16),
        compiler_params=pltpu.CompilerParams(dimension_semantics=("arbitrary",)),
    )(table, *blocks, *(other or []), hidden, out_grad, owner_ids.reshape(1, -1), doc_slot)


def local(hidden, out_grad, hidden_basis, output_basis, owner_ids, doc_slot):
    devices = lax.axis_size("dp")
    local_tokens = hidden.shape[0]
    capacity = 2 * local_tokens // devices
    rank_width = hidden_basis.shape[0]
    buffer_len = devices * capacity
    blocks, other, table = ring_gather(jnp.concatenate([hidden_basis, output_basis], axis=1), devices)
    packed = project_rows(blocks, other, table, hidden, out_grad, owner_ids, doc_slot, devices, capacity)
    arrived = lax.all_to_all(packed, "dp", 0, 0, tiled=True)
    rows_in = arrived[:, :capacity, :].reshape(buffer_len, 2 * rank_width)
    label_in = arrived[:, capacity, :capacity].reshape(buffer_len, 1)
    left_in = rows_in[:, :rank_width]
    right_in = rows_in[:, rank_width:]
    wanted = (jnp.arange(DOCS_DEV, dtype=jnp.int32) + 1).astype(jnp.bfloat16)[None, :]
    selector = (label_in == wanted).astype(jnp.bfloat16)
    weighted = (selector[:, :, None] * left_in[:, None, :]).reshape(buffer_len, DOCS_DEV * rank_width)
    grads = lax.dot_general(
        weighted, right_in, (((0,), (0,)), ((), ())), preferred_element_type=jnp.float32
    )
    return grads.reshape(DOCS_DEV, rank_width * rank_width)


def solution(mesh):
    placed = (
        P(("groups", "dp"), None),
        P(("groups", "dp"), None),
        P(None, "dp"),
        P(None, "dp"),
        P(("groups", "dp"), None),
        P(("groups", "dp")),
    )
    return jax.shard_map(
        local, mesh=mesh, in_specs=placed, out_specs=P(("groups", "dp"), None), check_vma=False
    )
```

```python
import numpy as np
import jax
import jax.numpy as jnp
from jax import lax
from jax.experimental import pallas as pl
from jax.experimental.pallas import tpu as pltpu
from jax.sharding import PartitionSpec as P

DOCS_DEV = 8


def ring_planes(devices):
    chips = devices // 2
    if devices % 2 or chips < 2:
        return [list(range(devices))]
    if chips % 2 == 0 and chips >= 4:
        order = list(range(0, chips, 2)) + list(range(chips - 1, 0, -2))
    else:
        order = list(range(chips))
    return [[2 * chip + core for chip in order] for core in range(2)]


def ring_gather(block, devices):
    planes = ring_planes(devices)
    length = len(planes[0])
    place = np.zeros(devices, np.int32)
    plane_of = np.zeros(devices, np.int32)
    for plane, members in enumerate(planes):
        for spot, member in enumerate(members):
            place[member] = spot
            plane_of[member] = plane
    forward = [(ring[t], ring[(t + 1) % length]) for ring in planes for t in range(length)]
    backward = [(ring[t], ring[(t - 1) % length]) for ring in planes for t in range(length)]
    early, late = [block], []
    early_shifts, late_shifts = [0], []
    split = max(1, length // 4)
    ahead = behind = block
    for step in range(1, length // 2 + 1):
        ahead = lax.ppermute(ahead, "dp", forward)
        (early if step <= split else late).append(ahead)
        (early_shifts if step <= split else late_shifts).append(-step)
        if step < length - length // 2:
            behind = lax.ppermute(behind, "dp", backward)
            (early if step <= split else late).append(behind)
            (early_shifts if step <= split else late_shifts).append(step)
    blocks = early + late
    shifts = early_shifts + late_shifts
    table = np.zeros((devices, len(shifts) * len(planes)), np.int32)
    for member in range(devices):
        for k, shift in enumerate(shifts):
            for side in range(len(planes)):
                ring = planes[(plane_of[member] + side) % len(planes)]
                table[member, side * len(shifts) + k] = ring[(place[member] + shift) % length]
    owners = jnp.asarray(table.reshape(-1))
    if len(planes) == 1:
        return blocks, None, owners
    swap = list(zip(planes[0], planes[1])) + list(zip(planes[1], planes[0]))
    other = [lax.ppermute(jnp.stack(group), "dp", swap) for group in (early, late) if group]
    return blocks, other, owners


def projection_kernel(count, devices, hidden_cols, output_cols, rank_width, paired, capacity):
    width = count * (2 if paired else 1)

    def kernel(table, *refs):
        blocks = refs[:count]
        rest = refs[count:]
        if paired:
            other_refs, rest = rest[:len(paired)], rest[len(paired):]
        hidden_ref, grad_ref, owner_ref, slot_ref, out_ref, rows, stacked, hidden_full, output_full = rest
        step = pl.program_id(0)
        tile = hidden_ref.shape[0]
        me = lax.axis_index("dp")

        @pl.when(step == 0)
        def _():
            for k in range(count):
                stacked[table[me * width + k]] = blocks[k][...]
            at = count
            for other_ref, size in zip(other_refs if paired else (), paired):
                for k in range(size):
                    stacked[table[me * width + at + k]] = other_ref[k]
                at += size
            for d in range(devices):
                hidden_full[:, d * hidden_cols:(d + 1) * hidden_cols] = stacked[d, :, output_cols:]
                output_full[:, d * output_cols:(d + 1) * output_cols] = stacked[d, :, :output_cols]

        dims = (((1,), (1,)), ((), ()))
        left = lax.dot_general(hidden_full[...], hidden_ref[...], dims, preferred_element_type=jnp.float32)
        right = lax.dot_general(output_full[...], grad_ref[...], dims, preferred_element_type=jnp.float32)
        at = pl.multiple_of(step * tile, tile)
        rows[:rank_width, pl.ds(at, tile)] = left.astype(jnp.bfloat16)
        rows[rank_width:, pl.ds(at, tile)] = right.astype(jnp.bfloat16)

        @pl.when(step == pl.num_programs(0) - 1)
        def _():
            lanes, tokens = rows.shape
            targets = owner_ref[...]
            slots = slot_ref[...].reshape(1, tokens)
            member = (targets == lax.broadcasted_iota(jnp.int32, (devices, tokens), 0)).astype(jnp.bfloat16)
            later = (
                lax.broadcasted_iota(jnp.int32, (tokens, tokens), 0)
                < lax.broadcasted_iota(jnp.int32, (tokens, tokens), 1)
            ).astype(jnp.bfloat16)
            before = jnp.dot(member, later, preferred_element_type=jnp.float32)
            position = jnp.sum(member.astype(jnp.float32) * before, axis=0, keepdims=True).astype(jnp.int32)
            slot_index = targets * capacity + position
            spread = (
                lax.broadcasted_iota(jnp.int32, (devices * capacity, tokens), 0) == slot_index
            ).astype(jnp.bfloat16)
            placed = lax.dot_general(spread, rows[...], dims, preferred_element_type=jnp.float32)
            placed = placed.astype(jnp.bfloat16)
            tagged = member * (slots + 1).astype(jnp.bfloat16)
            spot = (lax.broadcasted_iota(jnp.int32, (lanes, tokens), 0) == position).astype(jnp.bfloat16)
            labels = lax.dot_general(tagged, spot, dims, preferred_element_type=jnp.float32)
            labels = labels.astype(jnp.bfloat16)
            for d in range(devices):
                out_ref[d, :capacity, :] = placed[d * capacity:(d + 1) * capacity, :]
                out_ref[d, capacity:, :] = labels[d:d + 1, :]

    return kernel


def project_rows(blocks, other, table, hidden, out_grad, owner_ids, doc_slot, devices, capacity):
    count = len(blocks)
    paired = tuple(part.shape[0] for part in other) if other is not None else ()
    rank_width, width = blocks[0].shape
    local_tokens, features = hidden.shape
    outputs = out_grad.shape[1]
    tile = 128 if local_tokens % 128 == 0 else local_tokens
    whole = pl.BlockSpec((rank_width, width), lambda i, table: (0, 0))
    grid_spec = pltpu.PrefetchScalarGridSpec(
        num_scalar_prefetch=1,
        grid=(local_tokens // tile,),
        in_specs=[whole] * count + [pl.BlockSpec(part.shape, lambda i, table: (0, 0, 0)) for part in (other or [])] + [
            pl.BlockSpec((tile, features), lambda i, table: (i, 0)),
            pl.BlockSpec((tile, outputs), lambda i, table: (i, 0)),
            pl.BlockSpec((1, local_tokens), lambda i, table: (0, 0)),
            pl.BlockSpec((local_tokens,), lambda i, table: (0,)),
        ],
        out_specs=pl.BlockSpec((devices, capacity + 1, 2 * rank_width), lambda i, table: (0, 0, 0)),
        scratch_shapes=[
            pltpu.VMEM((2 * rank_width, local_tokens), jnp.bfloat16),
            pltpu.VMEM((devices, rank_width, width), jnp.bfloat16),
            pltpu.VMEM((rank_width, features), jnp.bfloat16),
            pltpu.VMEM((rank_width, outputs), jnp.bfloat16),
        ],
    )
    return pl.pallas_call(
        projection_kernel(count, devices, features // devices, outputs // devices, rank_width, paired, capacity),
        grid_spec=grid_spec,
        out_shape=jax.ShapeDtypeStruct((devices, capacity + 1, 2 * rank_width), jnp.bfloat16),
        compiler_params=pltpu.CompilerParams(dimension_semantics=("arbitrary",)),
    )(table, *blocks, *(other or []), hidden, out_grad, owner_ids.reshape(1, -1), doc_slot)


def local(hidden, out_grad, hidden_basis, output_basis, owner_ids, doc_slot):
    devices = lax.axis_size("dp")
    local_tokens = hidden.shape[0]
    capacity = 2 * local_tokens // devices
    rank_width = hidden_basis.shape[0]
    buffer_len = devices * capacity
    blocks, other, table = ring_gather(jnp.concatenate([output_basis, hidden_basis], axis=1), devices)
    packed = project_rows(blocks, other, table, hidden, out_grad, owner_ids, doc_slot, devices, capacity)
    arrived = lax.all_to_all(packed, "dp", 0, 0, tiled=True)
    rows_in = arrived[:, :capacity, :].reshape(buffer_len, 2 * rank_width)
    label_in = arrived[:, capacity, :capacity].reshape(buffer_len, 1)
    left_in = rows_in[:, :rank_width]
    right_in = rows_in[:, rank_width:]
    wanted = (jnp.arange(DOCS_DEV, dtype=jnp.int32) + 1).astype(jnp.bfloat16)[None, :]
    selector = (label_in == wanted).astype(jnp.bfloat16)
    weighted = (selector[:, :, None] * left_in[:, None, :]).reshape(buffer_len, DOCS_DEV * rank_width)
    grads = lax.dot_general(
        weighted, right_in, (((0,), (0,)), ((), ())), preferred_element_type=jnp.float32
    )
    return grads.reshape(DOCS_DEV, rank_width * rank_width)


def solution(mesh):
    placed = (
        P(("groups", "dp"), None),
        P(("groups", "dp"), None),
        P(None, "dp"),
        P(None, "dp"),
        P(("groups", "dp"), None),
        P(("groups", "dp")),
    )
    return jax.shard_map(
        local, mesh=mesh, in_specs=placed, out_specs=P(("groups", "dp"), None), check_vma=False
    )
```

```python
import numpy as np
import jax
import jax.numpy as jnp
from jax import lax
from jax.experimental import pallas as pl
from jax.experimental.pallas import tpu as pltpu
from jax.sharding import PartitionSpec as P

DOCS_DEV = 8


def ring_planes(devices):
    chips = devices // 2
    if devices % 2 or chips < 2:
        return [list(range(devices))]
    if chips % 2 == 0 and chips >= 4:
        order = list(range(0, chips, 2)) + list(range(chips - 1, 0, -2))
    else:
        order = list(range(chips))
    return [[2 * chip + core for chip in order] for core in range(2)]


def ring_gather(block, devices):
    planes = ring_planes(devices)
    length = len(planes[0])
    place = np.zeros(devices, np.int32)
    plane_of = np.zeros(devices, np.int32)
    for plane, members in enumerate(planes):
        for spot, member in enumerate(members):
            place[member] = spot
            plane_of[member] = plane
    forward = [(ring[t], ring[(t + 1) % length]) for ring in planes for t in range(length)]
    backward = [(ring[t], ring[(t - 1) % length]) for ring in planes for t in range(length)]
    early, late = [block], []
    early_shifts, late_shifts = [0], []
    split = max(1, length // 4)
    ahead = behind = block
    for step in range(1, length // 2 + 1):
        ahead = lax.ppermute(ahead, "dp", forward)
        (early if step <= split else late).append(ahead)
        (early_shifts if step <= split else late_shifts).append(-step)
        if step < length - length // 2:
            behind = lax.ppermute(behind, "dp", backward)
            (early if step <= split else late).append(behind)
            (early_shifts if step <= split else late_shifts).append(step)
    blocks = early + late
    shifts = early_shifts + late_shifts
    table = np.zeros((devices, len(shifts) * len(planes)), np.int32)
    for member in range(devices):
        for k, shift in enumerate(shifts):
            for side in range(len(planes)):
                ring = planes[(plane_of[member] + side) % len(planes)]
                table[member, side * len(shifts) + k] = ring[(place[member] + shift) % length]
    owners = jnp.asarray(table.reshape(-1))
    if len(planes) == 1:
        return blocks, None, owners
    swap = list(zip(planes[0], planes[1])) + list(zip(planes[1], planes[0]))
    other = [lax.ppermute(jnp.stack(group), "dp", swap) for group in (early, late) if group]
    return blocks, other, owners


def projection_kernel(count, devices, hidden_cols, output_cols, rank_width, paired, capacity):
    width = count * (2 if paired else 1)

    def kernel(table, *refs):
        blocks = refs[:count]
        rest = refs[count:]
        if paired:
            other_refs, rest = rest[:len(paired)], rest[len(paired):]
        hidden_ref, grad_ref, owner_ref, slot_ref, out_ref, rows, stacked, hidden_full, output_full = rest
        step = pl.program_id(0)
        tile = hidden_ref.shape[0]
        me = lax.axis_index("dp")

        @pl.when(step == 0)
        def _():
            for k in range(count):
                stacked[table[me * width + k]] = blocks[k][...]
            at = count
            for other_ref, size in zip(other_refs if paired else (), paired):
                for k in range(size):
                    stacked[table[me * width + at + k]] = other_ref[k]
                at += size
            for d in range(devices):
                hidden_full[:, d * hidden_cols:(d + 1) * hidden_cols] = stacked[d, :, :hidden_cols]
                output_full[:, d * output_cols:(d + 1) * output_cols] = stacked[d, :, hidden_cols:]

        dims = (((1,), (1,)), ((), ()))
        left = lax.dot_general(hidden_full[...], hidden_ref[...], dims, preferred_element_type=jnp.float32)
        right = lax.dot_general(output_full[...], grad_ref[...], dims, preferred_element_type=jnp.float32)
        at = pl.multiple_of(step * tile, tile)
        rows[:rank_width, pl.ds(at, tile)] = left.astype(jnp.bfloat16)
        rows[rank_width:, pl.ds(at, tile)] = right.astype(jnp.bfloat16)

        @pl.when(step == pl.num_programs(0) - 1)
        def _():
            lanes, tokens = rows.shape
            targets = owner_ref[...]
            slots = slot_ref[...].reshape(1, tokens)
            member = (targets == lax.broadcasted_iota(jnp.int32, (devices, tokens), 0)).astype(jnp.bfloat16)
            later = (
                lax.broadcasted_iota(jnp.int32, (tokens, tokens), 0)
                < lax.broadcasted_iota(jnp.int32, (tokens, tokens), 1)
            ).astype(jnp.bfloat16)
            before = jnp.dot(member, later, preferred_element_type=jnp.float32)
            position = jnp.sum(member.astype(jnp.float32) * before, axis=0, keepdims=True).astype(jnp.int32)
            slot_index = targets * capacity + position
            spread = (
                lax.broadcasted_iota(jnp.int32, (devices * capacity, tokens), 0) == slot_index
            ).astype(jnp.bfloat16)
            placed = lax.dot_general(spread, rows[...], dims, preferred_element_type=jnp.float32)
            placed = placed.astype(jnp.bfloat16)
            tagged = member * (slots + 1).astype(jnp.bfloat16)
            spot = (lax.broadcasted_iota(jnp.int32, (lanes, tokens), 0) == position).astype(jnp.bfloat16)
            labels = lax.dot_general(tagged, spot, dims, preferred_element_type=jnp.float32)
            labels = labels.astype(jnp.bfloat16)
            for d in range(devices):
                out_ref[d, :capacity, :] = placed[d * capacity:(d + 1) * capacity, :]
                out_ref[d, capacity:, :] = labels[d:d + 1, :]

    return kernel


def project_rows(blocks, other, table, hidden, out_grad, owner_ids, doc_slot, devices, capacity):
    count = len(blocks)
    paired = tuple(part.shape[0] for part in other) if other is not None else ()
    rank_width, width = blocks[0].shape
    local_tokens, features = hidden.shape
    outputs = out_grad.shape[1]
    tile = 128 if local_tokens % 128 == 0 else local_tokens
    whole = pl.BlockSpec((rank_width, width), lambda i, table: (0, 0))
    grid_spec = pltpu.PrefetchScalarGridSpec(
        num_scalar_prefetch=1,
        grid=(local_tokens // tile,),
        in_specs=[whole] * count + [pl.BlockSpec(part.shape, lambda i, table: (0, 0, 0)) for part in (other or [])] + [
            pl.BlockSpec((tile, features), lambda i, table: (i, 0)),
            pl.BlockSpec((tile, outputs), lambda i, table: (i, 0)),
            pl.BlockSpec((1, local_tokens), lambda i, table: (0, 0)),
            pl.BlockSpec((local_tokens,), lambda i, table: (0,)),
        ],
        out_specs=pl.BlockSpec((devices, capacity + 1, 2 * rank_width), lambda i, table: (0, 0, 0)),
        scratch_shapes=[
            pltpu.VMEM((2 * rank_width, local_tokens), jnp.bfloat16),
            pltpu.VMEM((devices, rank_width, width), jnp.bfloat16),
            pltpu.VMEM((rank_width, features), jnp.bfloat16),
            pltpu.VMEM((rank_width, outputs), jnp.bfloat16),
        ],
    )
    return pl.pallas_call(
        projection_kernel(count, devices, features // devices, outputs // devices, rank_width, paired, capacity),
        grid_spec=grid_spec,
        out_shape=jax.ShapeDtypeStruct((devices, capacity + 1, 2 * rank_width), jnp.bfloat16),
        compiler_params=pltpu.CompilerParams(dimension_semantics=("arbitrary",)),
    )(table, *blocks, *(other or []), hidden, out_grad, owner_ids.reshape(1, -1), doc_slot)


def local(hidden, out_grad, hidden_basis, output_basis, owner_ids, doc_slot):
    devices = lax.axis_size("dp")
    local_tokens = hidden.shape[0]
    capacity = 2 * local_tokens // devices
    rank_width = hidden_basis.shape[0]
    buffer_len = devices * capacity
    blocks, other, table = ring_gather(jnp.concatenate([hidden_basis, output_basis], axis=1), devices)
    packed = project_rows(blocks, other, table, hidden, out_grad, owner_ids, doc_slot, devices, capacity)
    arrived = lax.all_to_all(packed, "dp", 0, 0, tiled=True)
    rows_in = arrived[:, :capacity, :].reshape(buffer_len, 2 * rank_width)
    label_in = arrived[:, capacity, :capacity].reshape(buffer_len, 1)
    left_in = rows_in[:, :rank_width]
    right_in = rows_in[:, rank_width:]
    wanted = (jnp.arange(DOCS_DEV, dtype=jnp.int32) + 1).astype(jnp.bfloat16)[None, :]
    selector = (label_in == wanted).astype(jnp.bfloat16)
    weighted = (selector[:, :, None] * left_in[:, None, :]).reshape(buffer_len, DOCS_DEV * rank_width)
    return doc_grads(weighted, right_in, rank_width)


def doc_grads(weighted, right_in, rank_width):
    def kernel(weighted_ref, right_ref, out_ref, grads):
        grads[...] = lax.dot_general(
            weighted_ref[...], right_ref[...], (((0,), (0,)), ((), ())), preferred_element_type=jnp.float32
        )
        lanes = 2 * rank_width
        for pair in range(rank_width // 2):
            even = grads[pl.ds(2 * pair, DOCS_DEV, stride=rank_width), :]
            odd = grads[pl.ds(2 * pair + 1, DOCS_DEV, stride=rank_width), :]
            out_ref[:, pair * lanes:(pair + 1) * lanes] = jnp.concatenate([even, odd], axis=1)

    return pl.pallas_call(
        kernel,
        out_shape=jax.ShapeDtypeStruct((DOCS_DEV, rank_width * rank_width), jnp.float32),
        scratch_shapes=[pltpu.VMEM((DOCS_DEV * rank_width, rank_width), jnp.float32)],
    )(weighted, right_in)


def solution(mesh):
    placed = (
        P(("groups", "dp"), None),
        P(("groups", "dp"), None),
        P(None, "dp"),
        P(None, "dp"),
        P(("groups", "dp"), None),
        P(("groups", "dp")),
    )
    return jax.shard_map(
        local, mesh=mesh, in_specs=placed, out_specs=P(("groups", "dp"), None), check_vma=False
    )
```

```python
import numpy as np
import jax
import jax.numpy as jnp
from jax import lax
from jax.experimental import pallas as pl
from jax.experimental.pallas import tpu as pltpu
from jax.sharding import PartitionSpec as P

DOCS_DEV = 8


def ring_planes(devices):
    chips = devices // 2
    if devices % 2 or chips < 2:
        return [list(range(devices))]
    if chips % 2 == 0 and chips >= 4:
        order = list(range(0, chips, 2)) + list(range(chips - 1, 0, -2))
    else:
        order = list(range(chips))
    return [[2 * chip + core for chip in order] for core in range(2)]


def ring_gather(block, devices):
    planes = ring_planes(devices)
    length = len(planes[0])
    place = np.zeros(devices, np.int32)
    plane_of = np.zeros(devices, np.int32)
    for plane, members in enumerate(planes):
        for spot, member in enumerate(members):
            place[member] = spot
            plane_of[member] = plane
    forward = [(ring[t], ring[(t + 1) % length]) for ring in planes for t in range(length)]
    backward = [(ring[t], ring[(t - 1) % length]) for ring in planes for t in range(length)]
    cuts = (max(1, length // 8), max(1, length // 4))
    groups = [[block], [], []]
    group_shifts = [[0], [], []]
    ahead = behind = block
    for step in range(1, length // 2 + 1):
        group = sum(step > cut for cut in cuts)
        ahead = lax.ppermute(ahead, "dp", forward)
        groups[group].append(ahead)
        group_shifts[group].append(-step)
        if step < length - length // 2:
            behind = lax.ppermute(behind, "dp", backward)
            groups[group].append(behind)
            group_shifts[group].append(step)
    blocks = [got for group in groups for got in group]
    shifts = [shift for group in group_shifts for shift in group]
    table = np.zeros((devices, len(shifts) * len(planes)), np.int32)
    for member in range(devices):
        for k, shift in enumerate(shifts):
            for side in range(len(planes)):
                ring = planes[(plane_of[member] + side) % len(planes)]
                table[member, side * len(shifts) + k] = ring[(place[member] + shift) % length]
    owners = jnp.asarray(table.reshape(-1))
    if len(planes) == 1:
        return blocks, None, owners
    swap = list(zip(planes[0], planes[1])) + list(zip(planes[1], planes[0]))
    other = [lax.ppermute(jnp.stack(group), "dp", swap) for group in groups if group]
    return blocks, other, owners


def projection_kernel(count, devices, hidden_cols, output_cols, rank_width, paired, capacity):
    width = count * (2 if paired else 1)

    def kernel(table, *refs):
        blocks = refs[:count]
        rest = refs[count:]
        if paired:
            other_refs, rest = rest[:len(paired)], rest[len(paired):]
        hidden_ref, grad_ref, owner_ref, slot_ref, out_ref, rows, stacked, hidden_full, output_full = rest
        step = pl.program_id(0)
        tile = hidden_ref.shape[0]
        me = lax.axis_index("dp")

        @pl.when(step == 0)
        def _():
            for k in range(count):
                stacked[table[me * width + k]] = blocks[k][...]
            at = count
            for other_ref, size in zip(other_refs if paired else (), paired):
                for k in range(size):
                    stacked[table[me * width + at + k]] = other_ref[k]
                at += size
            for d in range(devices):
                hidden_full[:, d * hidden_cols:(d + 1) * hidden_cols] = stacked[d, :, :hidden_cols]
                output_full[:, d * output_cols:(d + 1) * output_cols] = stacked[d, :, hidden_cols:]

        dims = (((1,), (1,)), ((), ()))
        left = lax.dot_general(hidden_full[...], hidden_ref[...], dims, preferred_element_type=jnp.float32)
        right = lax.dot_general(output_full[...], grad_ref[...], dims, preferred_element_type=jnp.float32)
        at = pl.multiple_of(step * tile, tile)
        rows[:rank_width, pl.ds(at, tile)] = left.astype(jnp.bfloat16)
        rows[rank_width:, pl.ds(at, tile)] = right.astype(jnp.bfloat16)

        @pl.when(step == pl.num_programs(0) - 1)
        def _():
            lanes, tokens = rows.shape
            targets = owner_ref[...]
            slots = slot_ref[...].reshape(1, tokens)
            member = (targets == lax.broadcasted_iota(jnp.int32, (devices, tokens), 0)).astype(jnp.bfloat16)
            later = (
                lax.broadcasted_iota(jnp.int32, (tokens, tokens), 0)
                < lax.broadcasted_iota(jnp.int32, (tokens, tokens), 1)
            ).astype(jnp.bfloat16)
            before = jnp.dot(member, later, preferred_element_type=jnp.float32)
            position = jnp.sum(member.astype(jnp.float32) * before, axis=0, keepdims=True).astype(jnp.int32)
            slot_index = targets * capacity + position
            spread = (
                lax.broadcasted_iota(jnp.int32, (devices * capacity, tokens), 0) == slot_index
            ).astype(jnp.bfloat16)
            placed = lax.dot_general(spread, rows[...], dims, preferred_element_type=jnp.float32)
            placed = placed.astype(jnp.bfloat16)
            tagged = member * (slots + 1).astype(jnp.bfloat16)
            spot = (lax.broadcasted_iota(jnp.int32, (lanes, tokens), 0) == position).astype(jnp.bfloat16)
            labels = lax.dot_general(tagged, spot, dims, preferred_element_type=jnp.float32)
            labels = labels.astype(jnp.bfloat16)
            for d in range(devices):
                out_ref[d, :capacity, :] = placed[d * capacity:(d + 1) * capacity, :]
                out_ref[d, capacity:, :] = labels[d:d + 1, :]

    return kernel


def project_rows(blocks, other, table, hidden, out_grad, owner_ids, doc_slot, devices, capacity):
    count = len(blocks)
    paired = tuple(part.shape[0] for part in other) if other is not None else ()
    rank_width, width = blocks[0].shape
    local_tokens, features = hidden.shape
    outputs = out_grad.shape[1]
    tile = 128 if local_tokens % 128 == 0 else local_tokens
    whole = pl.BlockSpec((rank_width, width), lambda i, table: (0, 0))
    grid_spec = pltpu.PrefetchScalarGridSpec(
        num_scalar_prefetch=1,
        grid=(local_tokens // tile,),
        in_specs=[whole] * count + [pl.BlockSpec(part.shape, lambda i, table: (0, 0, 0)) for part in (other or [])] + [
            pl.BlockSpec((tile, features), lambda i, table: (i, 0)),
            pl.BlockSpec((tile, outputs), lambda i, table: (i, 0)),
            pl.BlockSpec((1, local_tokens), lambda i, table: (0, 0)),
            pl.BlockSpec((local_tokens,), lambda i, table: (0,)),
        ],
        out_specs=pl.BlockSpec((devices, capacity + 1, 2 * rank_width), lambda i, table: (0, 0, 0)),
        scratch_shapes=[
            pltpu.VMEM((2 * rank_width, local_tokens), jnp.bfloat16),
            pltpu.VMEM((devices, rank_width, width), jnp.bfloat16),
            pltpu.VMEM((rank_width, features), jnp.bfloat16),
            pltpu.VMEM((rank_width, outputs), jnp.bfloat16),
        ],
    )
    return pl.pallas_call(
        projection_kernel(count, devices, features // devices, outputs // devices, rank_width, paired, capacity),
        grid_spec=grid_spec,
        out_shape=jax.ShapeDtypeStruct((devices, capacity + 1, 2 * rank_width), jnp.bfloat16),
        compiler_params=pltpu.CompilerParams(dimension_semantics=("arbitrary",)),
    )(table, *blocks, *(other or []), hidden, out_grad, owner_ids.reshape(1, -1), doc_slot)


def local(hidden, out_grad, hidden_basis, output_basis, owner_ids, doc_slot):
    devices = lax.axis_size("dp")
    local_tokens = hidden.shape[0]
    capacity = 2 * local_tokens // devices
    rank_width = hidden_basis.shape[0]
    buffer_len = devices * capacity
    blocks, other, table = ring_gather(jnp.concatenate([hidden_basis, output_basis], axis=1), devices)
    packed = project_rows(blocks, other, table, hidden, out_grad, owner_ids, doc_slot, devices, capacity)
    arrived = lax.all_to_all(packed, "dp", 0, 0, tiled=True)
    rows_in = arrived[:, :capacity, :].reshape(buffer_len, 2 * rank_width)
    label_in = arrived[:, capacity, :capacity].reshape(buffer_len, 1)
    left_in = rows_in[:, :rank_width]
    right_in = rows_in[:, rank_width:]
    wanted = (jnp.arange(DOCS_DEV, dtype=jnp.int32) + 1).astype(jnp.bfloat16)[None, :]
    selector = (label_in == wanted).astype(jnp.bfloat16)
    weighted = (selector[:, :, None] * left_in[:, None, :]).reshape(buffer_len, DOCS_DEV * rank_width)
    grads = lax.dot_general(
        weighted, right_in, (((0,), (0,)), ((), ())), preferred_element_type=jnp.float32
    )
    return grads.reshape(DOCS_DEV, rank_width * rank_width)


def solution(mesh):
    placed = (
        P(("groups", "dp"), None),
        P(("groups", "dp"), None),
        P(None, "dp"),
        P(None, "dp"),
        P(("groups", "dp"), None),
        P(("groups", "dp")),
    )
    return jax.shard_map(
        local, mesh=mesh, in_specs=placed, out_specs=P(("groups", "dp"), None), check_vma=False
    )
```

```python
import numpy as np
import jax
import jax.numpy as jnp
from jax import lax
from jax.experimental import pallas as pl
from jax.experimental.pallas import tpu as pltpu
from jax.sharding import PartitionSpec as P

DOCS_DEV = 8


def ring_planes(devices):
    chips = devices // 2
    if devices % 2 or chips < 2:
        return [list(range(devices))]
    if chips % 2 == 0 and chips >= 4:
        order = list(range(0, chips, 2)) + list(range(chips - 1, 0, -2))
    else:
        order = list(range(chips))
    return [[2 * chip + core for chip in order] for core in range(2)]


def ring_gather(block, devices):
    planes = ring_planes(devices)
    length = len(planes[0])
    place = np.zeros(devices, np.int32)
    plane_of = np.zeros(devices, np.int32)
    for plane, members in enumerate(planes):
        for spot, member in enumerate(members):
            place[member] = spot
            plane_of[member] = plane
    forward = [(ring[t], ring[(t + 1) % length]) for ring in planes for t in range(length)]
    backward = [(ring[t], ring[(t - 1) % length]) for ring in planes for t in range(length)]
    early, late = [block], []
    early_shifts, late_shifts = [0], []
    split = max(1, length // 4)
    ahead = behind = block
    half = block.shape[0] // 2
    for step in range(1, length // 2 + 1):
        if step == length - step and half * 2 == block.shape[0] and step > 1:
            top = lax.ppermute(ahead[:half], "dp", forward)
            bottom = lax.ppermute(behind[half:], "dp", backward)
            late.append(jnp.concatenate([top, bottom], axis=0))
            late_shifts.append(-step)
            continue
        ahead = lax.ppermute(ahead, "dp", forward)
        (early if step <= split else late).append(ahead)
        (early_shifts if step <= split else late_shifts).append(-step)
        if step < length - length // 2:
            behind = lax.ppermute(behind, "dp", backward)
            (early if step <= split else late).append(behind)
            (early_shifts if step <= split else late_shifts).append(step)
    blocks = early + late
    shifts = early_shifts + late_shifts
    table = np.zeros((devices, len(shifts) * len(planes)), np.int32)
    for member in range(devices):
        for k, shift in enumerate(shifts):
            for side in range(len(planes)):
                ring = planes[(plane_of[member] + side) % len(planes)]
                table[member, side * len(shifts) + k] = ring[(place[member] + shift) % length]
    owners = jnp.asarray(table.reshape(-1))
    if len(planes) == 1:
        return blocks, None, owners
    swap = list(zip(planes[0], planes[1])) + list(zip(planes[1], planes[0]))
    other = [lax.ppermute(jnp.stack(group), "dp", swap) for group in (early, late) if group]
    return blocks, other, owners


def projection_kernel(count, devices, hidden_cols, output_cols, rank_width, paired, capacity):
    width = count * (2 if paired else 1)

    def kernel(table, *refs):
        blocks = refs[:count]
        rest = refs[count:]
        if paired:
            other_refs, rest = rest[:len(paired)], rest[len(paired):]
        hidden_ref, grad_ref, owner_ref, slot_ref, out_ref, rows, stacked, hidden_full, output_full = rest
        step = pl.program_id(0)
        tile = hidden_ref.shape[0]
        me = lax.axis_index("dp")

        @pl.when(step == 0)
        def _():
            for k in range(count):
                stacked[table[me * width + k]] = blocks[k][...]
            at = count
            for other_ref, size in zip(other_refs if paired else (), paired):
                for k in range(size):
                    stacked[table[me * width + at + k]] = other_ref[k]
                at += size
            for d in range(devices):
                hidden_full[:, d * hidden_cols:(d + 1) * hidden_cols] = stacked[d, :, :hidden_cols]
                output_full[:, d * output_cols:(d + 1) * output_cols] = stacked[d, :, hidden_cols:]

        dims = (((1,), (1,)), ((), ()))
        left = lax.dot_general(hidden_full[...], hidden_ref[...], dims, preferred_element_type=jnp.float32)
        right = lax.dot_general(output_full[...], grad_ref[...], dims, preferred_element_type=jnp.float32)
        at = pl.multiple_of(step * tile, tile)
        rows[:rank_width, pl.ds(at, tile)] = left.astype(jnp.bfloat16)
        rows[rank_width:, pl.ds(at, tile)] = right.astype(jnp.bfloat16)

        @pl.when(step == pl.num_programs(0) - 1)
        def _():
            lanes, tokens = rows.shape
            targets = owner_ref[...]
            slots = slot_ref[...].reshape(1, tokens)
            member = (targets == lax.broadcasted_iota(jnp.int32, (devices, tokens), 0)).astype(jnp.bfloat16)
            later = (
                lax.broadcasted_iota(jnp.int32, (tokens, tokens), 0)
                < lax.broadcasted_iota(jnp.int32, (tokens, tokens), 1)
            ).astype(jnp.bfloat16)
            before = jnp.dot(member, later, preferred_element_type=jnp.float32)
            position = jnp.sum(member.astype(jnp.float32) * before, axis=0, keepdims=True).astype(jnp.int32)
            slot_index = targets * capacity + position
            spread = (
                lax.broadcasted_iota(jnp.int32, (devices * capacity, tokens), 0) == slot_index
            ).astype(jnp.bfloat16)
            placed = lax.dot_general(spread, rows[...], dims, preferred_element_type=jnp.float32)
            placed = placed.astype(jnp.bfloat16)
            tagged = member * (slots + 1).astype(jnp.bfloat16)
            spot = (lax.broadcasted_iota(jnp.int32, (lanes, tokens), 0) == position).astype(jnp.bfloat16)
            labels = lax.dot_general(tagged, spot, dims, preferred_element_type=jnp.float32)
            labels = labels.astype(jnp.bfloat16)
            for d in range(devices):
                out_ref[d, :capacity, :] = placed[d * capacity:(d + 1) * capacity, :]
                out_ref[d, capacity:, :] = labels[d:d + 1, :]

    return kernel


def project_rows(blocks, other, table, hidden, out_grad, owner_ids, doc_slot, devices, capacity):
    count = len(blocks)
    paired = tuple(part.shape[0] for part in other) if other is not None else ()
    rank_width, width = blocks[0].shape
    local_tokens, features = hidden.shape
    outputs = out_grad.shape[1]
    tile = 128 if local_tokens % 128 == 0 else local_tokens
    whole = pl.BlockSpec((rank_width, width), lambda i, table: (0, 0))
    grid_spec = pltpu.PrefetchScalarGridSpec(
        num_scalar_prefetch=1,
        grid=(local_tokens // tile,),
        in_specs=[whole] * count + [pl.BlockSpec(part.shape, lambda i, table: (0, 0, 0)) for part in (other or [])] + [
            pl.BlockSpec((tile, features), lambda i, table: (i, 0)),
            pl.BlockSpec((tile, outputs), lambda i, table: (i, 0)),
            pl.BlockSpec((1, local_tokens), lambda i, table: (0, 0)),
            pl.BlockSpec((local_tokens,), lambda i, table: (0,)),
        ],
        out_specs=pl.BlockSpec((devices, capacity + 1, 2 * rank_width), lambda i, table: (0, 0, 0)),
        scratch_shapes=[
            pltpu.VMEM((2 * rank_width, local_tokens), jnp.bfloat16),
            pltpu.VMEM((devices, rank_width, width), jnp.bfloat16),
            pltpu.VMEM((rank_width, features), jnp.bfloat16),
            pltpu.VMEM((rank_width, outputs), jnp.bfloat16),
        ],
    )
    return pl.pallas_call(
        projection_kernel(count, devices, features // devices, outputs // devices, rank_width, paired, capacity),
        grid_spec=grid_spec,
        out_shape=jax.ShapeDtypeStruct((devices, capacity + 1, 2 * rank_width), jnp.bfloat16),
        compiler_params=pltpu.CompilerParams(dimension_semantics=("arbitrary",)),
    )(table, *blocks, *(other or []), hidden, out_grad, owner_ids.reshape(1, -1), doc_slot)


def local(hidden, out_grad, hidden_basis, output_basis, owner_ids, doc_slot):
    devices = lax.axis_size("dp")
    local_tokens = hidden.shape[0]
    capacity = 2 * local_tokens // devices
    rank_width = hidden_basis.shape[0]
    buffer_len = devices * capacity
    blocks, other, table = ring_gather(jnp.concatenate([hidden_basis, output_basis], axis=1), devices)
    packed = project_rows(blocks, other, table, hidden, out_grad, owner_ids, doc_slot, devices, capacity)
    arrived = lax.all_to_all(packed, "dp", 0, 0, tiled=True)
    rows_in = arrived[:, :capacity, :].reshape(buffer_len, 2 * rank_width)
    label_in = arrived[:, capacity, :capacity].reshape(buffer_len, 1)
    left_in = rows_in[:, :rank_width]
    right_in = rows_in[:, rank_width:]
    wanted = (jnp.arange(DOCS_DEV, dtype=jnp.int32) + 1).astype(jnp.bfloat16)[None, :]
    selector = (label_in == wanted).astype(jnp.bfloat16)
    weighted = (selector[:, :, None] * left_in[:, None, :]).reshape(buffer_len, DOCS_DEV * rank_width)
    grads = lax.dot_general(
        weighted, right_in, (((0,), (0,)), ((), ())), preferred_element_type=jnp.float32
    )
    return grads.reshape(DOCS_DEV, rank_width * rank_width)


def solution(mesh):
    placed = (
        P(("groups", "dp"), None),
        P(("groups", "dp"), None),
        P(None, "dp"),
        P(None, "dp"),
        P(("groups", "dp"), None),
        P(("groups", "dp")),
    )
    return jax.shard_map(
        local, mesh=mesh, in_specs=placed, out_specs=P(("groups", "dp"), None), check_vma=False
    )
```

```python
import numpy as np
import jax
import jax.numpy as jnp
from jax import lax
from jax.experimental import pallas as pl
from jax.experimental.pallas import tpu as pltpu
from jax.sharding import PartitionSpec as P

DOCS_DEV = 8


def ring_planes(devices):
    chips = devices // 2
    if devices % 2 or chips < 2:
        return [list(range(devices))]
    if chips % 2 == 0 and chips >= 4:
        order = list(range(0, chips, 2)) + list(range(chips - 1, 0, -2))
    else:
        order = list(range(chips))
    return [[2 * chip + core for chip in order] for core in range(2)]


def ring_gather(block, devices):
    planes = ring_planes(devices)
    length = len(planes[0])
    place = np.zeros(devices, np.int32)
    plane_of = np.zeros(devices, np.int32)
    for plane, members in enumerate(planes):
        for spot, member in enumerate(members):
            place[member] = spot
            plane_of[member] = plane
    forward = [(ring[t], ring[(t + 1) % length]) for ring in planes for t in range(length)]
    backward = [(ring[t], ring[(t - 1) % length]) for ring in planes for t in range(length)]
    early, late = [block], []
    early_shifts, late_shifts = [0], []
    split = max(1, length // 4)
    ahead = behind = block
    half = block.shape[0] // 2
    for step in range(1, length // 2 + 1):
        if step == length - step and half * 2 == block.shape[0] and step > 1:
            top = lax.ppermute(ahead[:half], "dp", forward)
            bottom = lax.ppermute(behind[half:], "dp", backward)
            late.append(jnp.concatenate([top, bottom], axis=0))
            late_shifts.append(-step)
            continue
        ahead = lax.ppermute(ahead, "dp", forward)
        (early if step <= split else late).append(ahead)
        (early_shifts if step <= split else late_shifts).append(-step)
        if step < length - length // 2:
            behind = lax.ppermute(behind, "dp", backward)
            (early if step <= split else late).append(behind)
            (early_shifts if step <= split else late_shifts).append(step)
    blocks = early + late
    shifts = early_shifts + late_shifts
    table = np.zeros((devices, len(shifts) * len(planes)), np.int32)
    for member in range(devices):
        for k, shift in enumerate(shifts):
            for side in range(len(planes)):
                ring = planes[(plane_of[member] + side) % len(planes)]
                table[member, side * len(shifts) + k] = ring[(place[member] + shift) % length]
    owners = jnp.asarray(table.reshape(-1))
    if len(planes) == 1:
        return blocks, None, owners
    swap = list(zip(planes[0], planes[1])) + list(zip(planes[1], planes[0]))
    other = [lax.ppermute(jnp.stack(group), "dp", swap) for group in (early, late) if group]
    return blocks, other, owners


def projection_kernel(count, devices, hidden_cols, output_cols, rank_width, paired, capacity):
    width = count * (2 if paired else 1)

    def kernel(table, *refs):
        blocks = refs[:count]
        rest = refs[count:]
        if paired:
            other_refs, rest = rest[:len(paired)], rest[len(paired):]
        hidden_ref, grad_ref, owner_ref, slot_ref, out_ref, rows, stacked, hidden_full, output_full = rest
        step = pl.program_id(0)
        tile = hidden_ref.shape[0]
        me = lax.axis_index("dp")

        @pl.when(step == 0)
        def _():
            for k in range(count):
                stacked[table[me * width + k]] = blocks[k][...]
            at = count
            for other_ref, size in zip(other_refs if paired else (), paired):
                for k in range(size):
                    stacked[table[me * width + at + k]] = other_ref[k]
                at += size
            for d in range(devices):
                hidden_full[:, d * hidden_cols:(d + 1) * hidden_cols] = stacked[d, :, output_cols:]
                output_full[:, d * output_cols:(d + 1) * output_cols] = stacked[d, :, :output_cols]

        dims = (((1,), (1,)), ((), ()))
        left = lax.dot_general(hidden_full[...], hidden_ref[...], dims, preferred_element_type=jnp.float32)
        right = lax.dot_general(output_full[...], grad_ref[...], dims, preferred_element_type=jnp.float32)
        at = pl.multiple_of(step * tile, tile)
        rows[:rank_width, pl.ds(at, tile)] = left.astype(jnp.bfloat16)
        rows[rank_width:, pl.ds(at, tile)] = right.astype(jnp.bfloat16)

        @pl.when(step == pl.num_programs(0) - 1)
        def _():
            lanes, tokens = rows.shape
            targets = owner_ref[...]
            slots = slot_ref[...].reshape(1, tokens)
            member = (targets == lax.broadcasted_iota(jnp.int32, (devices, tokens), 0)).astype(jnp.bfloat16)
            later = (
                lax.broadcasted_iota(jnp.int32, (tokens, tokens), 0)
                < lax.broadcasted_iota(jnp.int32, (tokens, tokens), 1)
            ).astype(jnp.bfloat16)
            before = jnp.dot(member, later, preferred_element_type=jnp.float32)
            position = jnp.sum(member.astype(jnp.float32) * before, axis=0, keepdims=True).astype(jnp.int32)
            slot_index = targets * capacity + position
            spread = (
                lax.broadcasted_iota(jnp.int32, (devices * capacity, tokens), 0) == slot_index
            ).astype(jnp.bfloat16)
            placed = lax.dot_general(spread, rows[...], dims, preferred_element_type=jnp.float32)
            placed = placed.astype(jnp.bfloat16)
            tagged = member * (slots + 1).astype(jnp.bfloat16)
            spot = (lax.broadcasted_iota(jnp.int32, (lanes, tokens), 0) == position).astype(jnp.bfloat16)
            labels = lax.dot_general(tagged, spot, dims, preferred_element_type=jnp.float32)
            labels = labels.astype(jnp.bfloat16)
            for d in range(devices):
                out_ref[d, :capacity, :] = placed[d * capacity:(d + 1) * capacity, :]
                out_ref[d, capacity:, :] = labels[d:d + 1, :]

    return kernel


def project_rows(blocks, other, table, hidden, out_grad, owner_ids, doc_slot, devices, capacity):
    count = len(blocks)
    paired = tuple(part.shape[0] for part in other) if other is not None else ()
    rank_width, width = blocks[0].shape
    local_tokens, features = hidden.shape
    outputs = out_grad.shape[1]
    tile = 128 if local_tokens % 128 == 0 else local_tokens
    whole = pl.BlockSpec((rank_width, width), lambda i, table: (0, 0))
    grid_spec = pltpu.PrefetchScalarGridSpec(
        num_scalar_prefetch=1,
        grid=(local_tokens // tile,),
        in_specs=[whole] * count + [pl.BlockSpec(part.shape, lambda i, table: (0, 0, 0)) for part in (other or [])] + [
            pl.BlockSpec((tile, features), lambda i, table: (i, 0)),
            pl.BlockSpec((tile, outputs), lambda i, table: (i, 0)),
            pl.BlockSpec((1, local_tokens), lambda i, table: (0, 0)),
            pl.BlockSpec((local_tokens,), lambda i, table: (0,)),
        ],
        out_specs=pl.BlockSpec((devices, capacity + 1, 2 * rank_width), lambda i, table: (0, 0, 0)),
        scratch_shapes=[
            pltpu.VMEM((2 * rank_width, local_tokens), jnp.bfloat16),
            pltpu.VMEM((devices, rank_width, width), jnp.bfloat16),
            pltpu.VMEM((rank_width, features), jnp.bfloat16),
            pltpu.VMEM((rank_width, outputs), jnp.bfloat16),
        ],
    )
    return pl.pallas_call(
        projection_kernel(count, devices, features // devices, outputs // devices, rank_width, paired, capacity),
        grid_spec=grid_spec,
        out_shape=jax.ShapeDtypeStruct((devices, capacity + 1, 2 * rank_width), jnp.bfloat16),
        compiler_params=pltpu.CompilerParams(dimension_semantics=("arbitrary",)),
    )(table, *blocks, *(other or []), hidden, out_grad, owner_ids.reshape(1, -1), doc_slot)


def local(hidden, out_grad, hidden_basis, output_basis, owner_ids, doc_slot):
    devices = lax.axis_size("dp")
    local_tokens = hidden.shape[0]
    capacity = 2 * local_tokens // devices
    rank_width = hidden_basis.shape[0]
    buffer_len = devices * capacity
    blocks, other, table = ring_gather(jnp.concatenate([output_basis, hidden_basis], axis=1), devices)
    packed = project_rows(blocks, other, table, hidden, out_grad, owner_ids, doc_slot, devices, capacity)
    arrived = lax.all_to_all(packed, "dp", 0, 0, tiled=True)
    rows_in = arrived[:, :capacity, :].reshape(buffer_len, 2 * rank_width)
    label_in = arrived[:, capacity, :capacity].reshape(buffer_len, 1)
    left_in = rows_in[:, :rank_width]
    right_in = rows_in[:, rank_width:]
    wanted = (jnp.arange(DOCS_DEV, dtype=jnp.int32) + 1).astype(jnp.bfloat16)[None, :]
    selector = (label_in == wanted).astype(jnp.bfloat16)
    weighted = (selector[:, :, None] * left_in[:, None, :]).reshape(buffer_len, DOCS_DEV * rank_width)
    grads = lax.dot_general(
        weighted, right_in, (((0,), (0,)), ((), ())), preferred_element_type=jnp.float32
    )
    return grads.reshape(DOCS_DEV, rank_width * rank_width)


def solution(mesh):
    placed = (
        P(("groups", "dp"), None),
        P(("groups", "dp"), None),
        P(None, "dp"),
        P(None, "dp"),
        P(("groups", "dp"), None),
        P(("groups", "dp")),
    )
    return jax.shard_map(
        local, mesh=mesh, in_specs=placed, out_specs=P(("groups", "dp"), None), check_vma=False
    )
```

```python
import numpy as np
import jax
import jax.numpy as jnp
from jax import lax
from jax.experimental import pallas as pl
from jax.experimental.pallas import tpu as pltpu
from jax.sharding import PartitionSpec as P

DOCS_DEV = 8


def ring_planes(devices):
    chips = devices // 2
    if devices % 2 or chips < 2:
        return [list(range(devices))]
    if chips % 2 == 0 and chips >= 4:
        order = list(range(0, chips, 2)) + list(range(chips - 1, 0, -2))
    else:
        order = list(range(chips))
    return [[2 * chip + core for chip in order] for core in range(2)]


def ring_gather(block, devices):
    planes = ring_planes(devices)
    length = len(planes[0])
    place = np.zeros(devices, np.int32)
    plane_of = np.zeros(devices, np.int32)
    for plane, members in enumerate(planes):
        for spot, member in enumerate(members):
            place[member] = spot
            plane_of[member] = plane
    forward = [(ring[t], ring[(t + 1) % length]) for ring in planes for t in range(length)]
    backward = [(ring[t], ring[(t - 1) % length]) for ring in planes for t in range(length)]
    early, late = [block], []
    early_shifts, late_shifts = [0], []
    split = max(1, length // 8)
    ahead = behind = block
    for step in range(1, length // 2 + 1):
        ahead = lax.ppermute(ahead, "dp", forward)
        (early if step <= split else late).append(ahead)
        (early_shifts if step <= split else late_shifts).append(-step)
        if step < length - length // 2:
            behind = lax.ppermute(behind, "dp", backward)
            (early if step <= split else late).append(behind)
            (early_shifts if step <= split else late_shifts).append(step)
    blocks = early + late
    shifts = early_shifts + late_shifts
    table = np.zeros((devices, len(shifts) * len(planes)), np.int32)
    for member in range(devices):
        for k, shift in enumerate(shifts):
            for side in range(len(planes)):
                ring = planes[(plane_of[member] + side) % len(planes)]
                table[member, side * len(shifts) + k] = ring[(place[member] + shift) % length]
    owners = jnp.asarray(table.reshape(-1))
    if len(planes) == 1:
        return blocks, None, owners
    swap = list(zip(planes[0], planes[1])) + list(zip(planes[1], planes[0]))
    other = [lax.ppermute(jnp.stack(group), "dp", swap) for group in (early, late) if group]
    return blocks, other, owners


def projection_kernel(count, devices, hidden_cols, output_cols, rank_width, paired, capacity):
    width = count * (2 if paired else 1)

    def kernel(table, *refs):
        blocks = refs[:count]
        rest = refs[count:]
        if paired:
            other_refs, rest = rest[:len(paired)], rest[len(paired):]
        hidden_ref, grad_ref, owner_ref, slot_ref, out_ref, rows, stacked, hidden_full, output_full = rest
        step = pl.program_id(0)
        tile = hidden_ref.shape[0]
        me = lax.axis_index("dp")

        @pl.when(step == 0)
        def _():
            for k in range(count):
                stacked[table[me * width + k]] = blocks[k][...]
            at = count
            for other_ref, size in zip(other_refs if paired else (), paired):
                for k in range(size):
                    stacked[table[me * width + at + k]] = other_ref[k]
                at += size
            for d in range(devices):
                hidden_full[:, d * hidden_cols:(d + 1) * hidden_cols] = stacked[d, :, :hidden_cols]
                output_full[:, d * output_cols:(d + 1) * output_cols] = stacked[d, :, hidden_cols:]

        dims = (((1,), (1,)), ((), ()))
        left = lax.dot_general(hidden_full[...], hidden_ref[...], dims, preferred_element_type=jnp.float32)
        right = lax.dot_general(output_full[...], grad_ref[...], dims, preferred_element_type=jnp.float32)
        at = pl.multiple_of(step * tile, tile)
        rows[:rank_width, pl.ds(at, tile)] = left.astype(jnp.bfloat16)
        rows[rank_width:, pl.ds(at, tile)] = right.astype(jnp.bfloat16)

        @pl.when(step == pl.num_programs(0) - 1)
        def _():
            lanes, tokens = rows.shape
            targets = owner_ref[...]
            slots = slot_ref[...].reshape(1, tokens)
            member = (targets == lax.broadcasted_iota(jnp.int32, (devices, tokens), 0)).astype(jnp.bfloat16)
            later = (
                lax.broadcasted_iota(jnp.int32, (tokens, tokens), 0)
                < lax.broadcasted_iota(jnp.int32, (tokens, tokens), 1)
            ).astype(jnp.bfloat16)
            before = jnp.dot(member, later, preferred_element_type=jnp.float32)
            position = jnp.sum(member.astype(jnp.float32) * before, axis=0, keepdims=True).astype(jnp.int32)
            slot_index = targets * capacity + position
            spread = (
                lax.broadcasted_iota(jnp.int32, (devices * capacity, tokens), 0) == slot_index
            ).astype(jnp.bfloat16)
            placed = lax.dot_general(spread, rows[...], dims, preferred_element_type=jnp.float32)
            placed = placed.astype(jnp.bfloat16)
            tagged = member * (slots + 1).astype(jnp.bfloat16)
            spot = (lax.broadcasted_iota(jnp.int32, (lanes, tokens), 0) == position).astype(jnp.bfloat16)
            labels = lax.dot_general(tagged, spot, dims, preferred_element_type=jnp.float32)
            labels = labels.astype(jnp.bfloat16)
            for d in range(devices):
                out_ref[d, :capacity, :] = placed[d * capacity:(d + 1) * capacity, :]
                out_ref[d, capacity:, :] = labels[d:d + 1, :]

    return kernel


def project_rows(blocks, other, table, hidden, out_grad, owner_ids, doc_slot, devices, capacity):
    count = len(blocks)
    paired = tuple(part.shape[0] for part in other) if other is not None else ()
    rank_width, width = blocks[0].shape
    local_tokens, features = hidden.shape
    outputs = out_grad.shape[1]
    tile = 128 if local_tokens % 128 == 0 else local_tokens
    whole = pl.BlockSpec((rank_width, width), lambda i, table: (0, 0))
    grid_spec = pltpu.PrefetchScalarGridSpec(
        num_scalar_prefetch=1,
        grid=(local_tokens // tile,),
        in_specs=[whole] * count + [pl.BlockSpec(part.shape, lambda i, table: (0, 0, 0)) for part in (other or [])] + [
            pl.BlockSpec((tile, features), lambda i, table: (i, 0)),
            pl.BlockSpec((tile, outputs), lambda i, table: (i, 0)),
            pl.BlockSpec((1, local_tokens), lambda i, table: (0, 0)),
            pl.BlockSpec((local_tokens,), lambda i, table: (0,)),
        ],
        out_specs=pl.BlockSpec((devices, capacity + 1, 2 * rank_width), lambda i, table: (0, 0, 0)),
        scratch_shapes=[
            pltpu.VMEM((2 * rank_width, local_tokens), jnp.bfloat16),
            pltpu.VMEM((devices, rank_width, width), jnp.bfloat16),
            pltpu.VMEM((rank_width, features), jnp.bfloat16),
            pltpu.VMEM((rank_width, outputs), jnp.bfloat16),
        ],
    )
    return pl.pallas_call(
        projection_kernel(count, devices, features // devices, outputs // devices, rank_width, paired, capacity),
        grid_spec=grid_spec,
        out_shape=jax.ShapeDtypeStruct((devices, capacity + 1, 2 * rank_width), jnp.bfloat16),
        compiler_params=pltpu.CompilerParams(dimension_semantics=("arbitrary",)),
    )(table, *blocks, *(other or []), hidden, out_grad, owner_ids.reshape(1, -1), doc_slot)


def local(hidden, out_grad, hidden_basis, output_basis, owner_ids, doc_slot):
    devices = lax.axis_size("dp")
    local_tokens = hidden.shape[0]
    capacity = 2 * local_tokens // devices
    rank_width = hidden_basis.shape[0]
    buffer_len = devices * capacity
    blocks, other, table = ring_gather(jnp.concatenate([hidden_basis, output_basis], axis=1), devices)
    packed = project_rows(blocks, other, table, hidden, out_grad, owner_ids, doc_slot, devices, capacity)
    arrived = lax.all_to_all(packed, "dp", 0, 0, tiled=True)
    rows_in = arrived[:, :capacity, :].reshape(buffer_len, 2 * rank_width)
    label_in = arrived[:, capacity, :capacity].reshape(buffer_len, 1)
    left_in = rows_in[:, :rank_width]
    right_in = rows_in[:, rank_width:]
    wanted = (jnp.arange(DOCS_DEV, dtype=jnp.int32) + 1).astype(jnp.bfloat16)[None, :]
    selector = (label_in == wanted).astype(jnp.bfloat16)
    weighted = (selector[:, :, None] * left_in[:, None, :]).reshape(buffer_len, DOCS_DEV * rank_width)
    grads = lax.dot_general(
        weighted, right_in, (((0,), (0,)), ((), ())), preferred_element_type=jnp.float32
    )
    return grads.reshape(DOCS_DEV, rank_width * rank_width)


def solution(mesh):
    placed = (
        P(("groups", "dp"), None),
        P(("groups", "dp"), None),
        P(None, "dp"),
        P(None, "dp"),
        P(("groups", "dp"), None),
        P(("groups", "dp")),
    )
    return jax.shard_map(
        local, mesh=mesh, in_specs=placed, out_specs=P(("groups", "dp"), None), check_vma=False
    )
```
